256 devices in a mesh: seq: 64 (over x, z_lo, y, core), mp: 4 (over z_hi).
Axes of the slice: x: 4, y: 4, z: 8 (z_hi: 4, z_lo: 2; z = z_hi * 2 + z_lo), core: 2. Of those that a mesh axis runs over, the one named last changes fastest.
Arguments:
- tokens: bfloat16 [8192, 4096], P('seq', 'mp'), may hold values from -6 to 6
- w_proj: bfloat16 [4096, 3, 2048], P('seq', None, 'mp'), may hold values from -0.09375 to 0.09375
- short_filter: float32 [3, 3, 2048], P(None, None, 'mp'), may hold values from -3.5 to 3.5
- long_filter: float32 [2048, 8192], P(('mp', 'seq')), may hold values from -0.0625 to 0.0625
- skip_gain: float32 [2048], P('mp'), may hold values from -4 to 4
Outputs:
- gated: bfloat16 [8192, 2048], P('seq', 'mp')
The draws below stay inside these ranges and needn't reach their ends.
All inputs are finite; a program needn't handle non-finite values.
Results may differ from the reference program's by a relative error of at most 0.012.
Values may be sent and summed in bfloat16 or wider, within the bound.
No kernel may reach another device: no remote copies, remote signals or barrier semaphores. Data moves between devices by JAX's collectives and lax.ppermute only.
A program may use at most 64 MiB of HBM per device.

```python
import math
import jax
import jax.numpy as jnp
from jax import lax

D = 4096
CH = 2048
KS = 3
SEQLEN = 8192


def levels(own_key, dims, shards, least, high):
    level, own = 1.0, jax.random.fold_in(own_key, 6)
    for position, blocks in shards:
        steps = jnp.exp(jax.random.uniform(jax.random.fold_in(own, position), (blocks,), jnp.float32, least / len(shards), high / len(shards)))
        level = level * jnp.repeat(steps, dims[position] // blocks).reshape([-1 if axis == position else 1 for axis in range(len(dims))])
    return level


def noise(key, extent, deviation, bound, shards=(), kind=jnp.bfloat16):
    loudness = levels(key, extent, shards, -0.22, 0.18) if shards else 1.0
    entries = jax.random.normal(key, extent, jnp.float32) * deviation * loudness
    return jnp.minimum(jnp.maximum(entries, -bound), bound).astype(kind)


def setup_inputs(seed: int = 0) -> dict:
    keys = jax.random.split(jax.random.key(seed), 6)
    tokens = noise(keys[0], (SEQLEN, D), 1.0, 6.0, ((0, 64), (1, 4)))
    w_proj = noise(keys[1], (D, 3, CH), D ** -0.5, 0.09375, ((0, 64), (2, 4)))
    short_filter = noise(keys[2], (3, KS, CH), KS ** -0.5, 3.5, ((2, 4),), jnp.float32)
    long_filter = noise(keys[3], (CH, SEQLEN), SEQLEN ** -0.5, 0.0625, ((0, 256),), jnp.float32)
    skip_gain = noise(keys[4], (CH,), 1.0, 4.0, ((0, 4),), jnp.float32)
    return dict(tokens=tokens, w_proj=w_proj, short_filter=short_filter, long_filter=long_filter, skip_gain=skip_gain)


def reference(tokens, w_proj, short_filter, long_filter, skip_gain):
    branches = []
    for member in range(3):
        projected = jnp.dot(tokens, w_proj[:, member, :], preferred_element_type=jnp.float32).astype(jnp.bfloat16)
        padded = jnp.pad(projected.astype(jnp.float32), ((KS - 1, 0), (0, 0)))
        mixed = jnp.zeros((SEQLEN, CH), jnp.float32)
        for offset in range(KS):
            mixed = mixed + short_filter[member, offset][None, :] * padded[KS - 1 - offset:KS - 1 - offset + SEQLEN]
        branches.append(mixed)
    query_rows, key_rows, value_rows = branches
    product = (key_rows * value_rows).astype(jnp.bfloat16)
    blocked = math.gcd(CH, 128)
    channel_major = product.astype(jnp.float32).T.reshape(CH // blocked, blocked, SEQLEN)
    filter_major = long_filter.reshape(CH // blocked, blocked, SEQLEN)
    padded_len = 2 * SEQLEN

    def convolve(pair):
        signal, kernel = pair
        spectrum = jnp.fft.rfft(signal, n=padded_len) * jnp.fft.rfft(kernel, n=padded_len)
        return jnp.fft.irfft(spectrum, n=padded_len)[:, :SEQLEN]

    convolved = lax.map(convolve, (channel_major, filter_major)).reshape(CH, SEQLEN).T.astype(jnp.bfloat16)
    result = query_rows * (convolved.astype(jnp.float32) + skip_gain[None, :] * product.astype(jnp.float32))
    return result.astype(jnp.bfloat16)
```

```python
import numpy as np

import jax
import jax.numpy as jnp
from jax import lax
from jax.sharding import PartitionSpec as P

HIGHEST = lax.Precision.HIGHEST


def shifted(value, axis, steps):
    count = lax.axis_size(axis)
    leading, last = (max(0, -steps), min(count, count - steps))
    return lax.ppermute(value, axis, [(source, source + steps) for source in range(leading, last)])


def tables(rows, cols):
    first = np.arange(rows)
    second = np.arange(cols)
    outer = 2.0 * np.pi * np.outer(first, first) / rows
    inner = 2.0 * np.pi * np.outer(second, second) / cols
    twist = 2.0 * np.pi * np.outer(first, second) / (rows * cols)
    f32 = lambda a: jnp.asarray(a.astype(np.float32))
    return dict(
        outer_cos=f32(np.cos(outer)),
        outer_sin=f32(np.sin(outer)),
        inner_cos=f32(np.cos(inner)),
        inner_sin=f32(np.sin(inner)),
        twist_cos=f32(np.cos(twist)),
        twist_sin=f32(np.sin(twist)),
    )


def forward(first_re, first_im, t):
    tc = t["twist_cos"][:, None, :]
    ts = t["twist_sin"][:, None, :]
    b_re = first_re * tc + first_im * ts
    b_im = first_im * tc - first_re * ts
    dot = lambda a, m: jnp.einsum("krn,nm->krm", a, m, precision=HIGHEST)
    x_re = dot(b_re, t["inner_cos"]) + dot(b_im, t["inner_sin"])
    x_im = dot(b_im, t["inner_cos"]) - dot(b_re, t["inner_sin"])
    return x_re, x_im


def long_conv(signal, kernel):
    live, channels, cols = signal.shape
    rows = 2 * live
    t = tables(rows, cols)
    oc = t["outer_cos"][:, :live]
    os_ = t["outer_sin"][:, :live]
    sig = signal.astype(jnp.float32)
    s_re = jnp.einsum("kn,nrm->krm", oc, sig, precision=HIGHEST)
    s_im = -jnp.einsum("kn,nrm->krm", os_, sig, precision=HIGHEST)
    ker = kernel.reshape(channels, live, cols)
    h_re = jnp.einsum("kn,rnm->krm", oc, ker, precision=HIGHEST)
    h_im = -jnp.einsum("kn,rnm->krm", os_, ker, precision=HIGHEST)
    su_re, su_im = forward(s_re, s_im, t)
    sh_re, sh_im = forward(h_re, h_im, t)
    z_re = su_re * sh_re - su_im * sh_im
    z_im = su_re * sh_im + su_im * sh_re
    dot = lambda a, m: jnp.einsum("krn,nm->krm", a, m, precision=HIGHEST)
    d_re = dot(z_re, t["inner_cos"]) - dot(z_im, t["inner_sin"])
    d_im = dot(z_im, t["inner_cos"]) + dot(z_re, t["inner_sin"])
    tc = t["twist_cos"][:, None, :]
    ts = t["twist_sin"][:, None, :]
    e_re = d_re * tc - d_im * ts
    e_im = d_im * tc + d_re * ts
    scale = 1.0 / (rows * cols)
    back_cos = t["outer_cos"][:live] * scale
    back_sin = t["outer_sin"][:live] * scale
    return jnp.einsum("nk,krm->nrm", back_cos, e_re, precision=HIGHEST) - jnp.einsum(
        "nk,krm->nrm", back_sin, e_im, precision=HIGHEST
    )


def on_device(tokens, w_proj, short_filter, long_filter, skip_gain):
    rows_dev = tokens.shape[0]
    margin = short_filter.shape[1] - 1
    width = w_proj.shape[2]
    source = lax.all_gather(tokens, "mp", axis=1, tiled=True)
    projected = jnp.einsum(
        "td,dpc->tpc",
        source,
        lax.all_gather(w_proj, "seq", axis=0, tiled=True),
        preferred_element_type=jnp.float32,
    ).astype(jnp.bfloat16)
    tail = shifted(projected[rows_dev - margin :], "seq", 1)
    extended = jnp.concatenate([tail, projected], axis=0).astype(jnp.float32)
    mixed = jnp.zeros((rows_dev, 3, width), jnp.float32)
    for offset in range(margin + 1):
        mixed = (
            mixed
            + short_filter[:, offset, :][None]
            * extended[margin - offset : margin - offset + rows_dev]
        )
    query_rows = mixed[:, 0]
    product = (mixed[:, 1] * mixed[:, 2]).astype(jnp.bfloat16)
    groups = lax.axis_size("seq")
    channel_count = width // groups
    outgoing = product.T.reshape(groups, channel_count, rows_dev)
    arrived = lax.all_to_all(outgoing, "seq", split_axis=0, concat_axis=0, tiled=True)
    convolved = long_conv(arrived, long_filter).astype(jnp.bfloat16)
    returned = lax.all_to_all(convolved, "seq", split_axis=0, concat_axis=0, tiled=True)
    back_rows = returned.reshape(width, rows_dev).T
    result = query_rows * (
        back_rows.astype(jnp.float32) + skip_gain[None, :] * product.astype(jnp.float32)
    )
    return result.astype(jnp.bfloat16)


def solution(mesh):
    return jax.shard_map(
        on_device,
        mesh=mesh,
        in_specs=(
            P("seq", "mp"),
            P("seq", None, "mp"),
            P(None, None, "mp"),
            P(("mp", "seq"), None),
            P("mp"),
        ),
        out_specs=P("seq", "mp"),
        check_vma=False,
    )
```

```python
import numpy as np

import jax
import jax.numpy as jnp
from jax import lax
from jax.sharding import PartitionSpec as P

HIGHEST = lax.Precision.HIGHEST
GROUP = 8


def shifted(value, axis, steps):
    count = lax.axis_size(axis)
    leading, last = (max(0, -steps), min(count, count - steps))
    return lax.ppermute(value, axis, [(source, source + steps) for source in range(leading, last)])


def tables(rows, cols):
    first = np.arange(rows)
    second = np.arange(cols)
    outer = 2.0 * np.pi * np.outer(first, first) / rows
    inner = 2.0 * np.pi * np.outer(second, second) / cols
    twist = 2.0 * np.pi * np.outer(first, second) / (rows * cols)
    f32 = lambda a: jnp.asarray(a.astype(np.float32))
    return dict(
        outer_cos=f32(np.cos(outer)),
        outer_sin=f32(np.sin(outer)),
        inner_cos=f32(np.cos(inner)),
        inner_sin=f32(np.sin(inner)),
        twist_cos=f32(np.cos(twist)),
        twist_sin=f32(np.sin(twist)),
    )


def forward(first_re, first_im, t):
    tc = t["twist_cos"][:, None, :]
    ts = t["twist_sin"][:, None, :]
    b_re = first_re * tc + first_im * ts
    b_im = first_im * tc - first_re * ts
    dot = lambda a, m: jnp.einsum("krn,nm->krm", a, m, precision=HIGHEST)
    x_re = dot(b_re, t["inner_cos"]) + dot(b_im, t["inner_sin"])
    x_im = dot(b_im, t["inner_cos"]) - dot(b_re, t["inner_sin"])
    return x_re, x_im


def long_conv(signal, kernel):
    live, channels, cols = signal.shape
    rows = 2 * live
    t = tables(rows, cols)
    oc = t["outer_cos"][:, :live]
    os_ = t["outer_sin"][:, :live]
    sig = signal.astype(jnp.float32)
    s_re = jnp.einsum("kn,nrm->krm", oc, sig, precision=HIGHEST)
    s_im = -jnp.einsum("kn,nrm->krm", os_, sig, precision=HIGHEST)
    ker = kernel.reshape(channels, live, cols)
    h_re = jnp.einsum("kn,rnm->krm", oc, ker, precision=HIGHEST)
    h_im = -jnp.einsum("kn,rnm->krm", os_, ker, precision=HIGHEST)
    su_re, su_im = forward(s_re, s_im, t)
    sh_re, sh_im = forward(h_re, h_im, t)
    z_re = su_re * sh_re - su_im * sh_im
    z_im = su_re * sh_im + su_im * sh_re
    dot = lambda a, m: jnp.einsum("krn,nm->krm", a, m, precision=HIGHEST)
    d_re = dot(z_re, t["inner_cos"]) - dot(z_im, t["inner_sin"])
    d_im = dot(z_im, t["inner_cos"]) + dot(z_re, t["inner_sin"])
    tc = t["twist_cos"][:, None, :]
    ts = t["twist_sin"][:, None, :]
    e_re = d_re * tc - d_im * ts
    e_im = d_im * tc + d_re * ts
    scale = 1.0 / (rows * cols)
    back_cos = t["outer_cos"][:live] * scale
    back_sin = t["outer_sin"][:live] * scale
    return jnp.einsum("nk,krm->nrm", back_cos, e_re, precision=HIGHEST) - jnp.einsum(
        "nk,krm->nrm", back_sin, e_im, precision=HIGHEST
    )


def pick(values, axis, parity):
    shape = values.shape
    grouped = values.reshape(shape[:axis] + (shape[axis] // (2 * GROUP), 2, GROUP) + shape[axis + 1 :])
    taken = lax.dynamic_index_in_dim(grouped, parity, axis + 1, keepdims=False)
    return taken.reshape(shape[:axis] + (shape[axis] // 2,) + shape[axis + 1 :])


def on_device(tokens, w_proj, short_filter, long_filter, skip_gain):
    rows_dev = tokens.shape[0]
    margin = short_filter.shape[1] - 1
    width = w_proj.shape[2]
    half = width // 2
    chips = lax.axis_size("chip")
    parity = lax.axis_index("core")
    source = lax.all_gather(lax.all_gather(tokens, "mp", axis=1, tiled=True), "core", axis=0, tiled=True)
    split = w_proj.reshape(w_proj.shape[0], 3, width // (2 * GROUP), 2, GROUP)
    split = jnp.moveaxis(split, 3, 0).reshape(2, w_proj.shape[0], 3, half)
    paired = lax.all_to_all(split, "core", split_axis=0, concat_axis=0, tiled=True)
    weights = lax.all_gather(paired.reshape(2 * w_proj.shape[0], 3, half), "chip", axis=0, tiled=True)
    projected = jnp.einsum(
        "td,dpc->tpc", source, weights, preferred_element_type=jnp.float32
    ).astype(jnp.bfloat16)
    rows = source.shape[0]
    tail = shifted(projected[rows - margin :], "chip", 1)
    extended = jnp.concatenate([tail, projected], axis=0).astype(jnp.float32)
    taps = pick(short_filter, 2, parity)
    mixed = jnp.zeros((rows, 3, half), jnp.float32)
    for offset in range(margin + 1):
        mixed = mixed + taps[:, offset, :][None] * extended[margin - offset : margin - offset + rows]
    query_rows = mixed[:, 0]
    product = (mixed[:, 1] * mixed[:, 2]).astype(jnp.bfloat16)
    outgoing = product.T.reshape(chips, GROUP, rows)
    arrived = lax.all_to_all(outgoing, "chip", split_axis=0, concat_axis=0, tiled=True)
    convolved = long_conv(arrived, long_filter).astype(jnp.bfloat16)
    returned = lax.all_to_all(convolved, "chip", split_axis=0, concat_axis=0, tiled=True)
    back_rows = returned.reshape(half, rows).T
    gain = pick(skip_gain, 0, parity)
    local = query_rows * (back_rows.astype(jnp.float32) + gain[None, :] * product.astype(jnp.float32))
    local = local.astype(jnp.bfloat16).reshape(2, rows_dev, half)
    swapped = lax.all_to_all(local, "core", split_axis=0, concat_axis=0, tiled=True)
    swapped = swapped.reshape(2, rows_dev, half // GROUP, GROUP)
    return jnp.transpose(swapped, (1, 2, 0, 3)).reshape(rows_dev, width)


def solution(mesh):
    seq_size = mesh.shape["seq"]
    devices = mesh.devices.reshape(seq_size // 2, 2, mesh.shape["mp"])
    inner = jax.sharding.Mesh(devices, ("chip", "core", "mp"))
    seq = ("chip", "core")
    return jax.shard_map(
        on_device,
        mesh=inner,
        in_specs=(
            P(seq, "mp"),
            P(seq, None, "mp"),
            P(None, None, "mp"),
            P(("mp",) + seq, None),
            P("mp"),
        ),
        out_specs=P(seq, "mp"),
        check_vma=False,
    )
```

```python
import numpy as np

import jax
import jax.numpy as jnp
from jax import lax
from jax.sharding import PartitionSpec as P

HIGHEST = lax.Precision.HIGHEST
GROUP = 8


def shifted(value, axis, steps):
    count = lax.axis_size(axis)
    leading, last = (max(0, -steps), min(count, count - steps))
    return lax.ppermute(value, axis, [(source, source + steps) for source in range(leading, last)])


def tables(rows, cols):
    first = np.arange(rows)
    second = np.arange(cols)
    outer = 2.0 * np.pi * np.outer(first, first) / rows
    inner = 2.0 * np.pi * np.outer(second, second) / cols
    twist = 2.0 * np.pi * np.outer(first, second) / (rows * cols)
    f32 = lambda a: jnp.asarray(a.astype(np.float32))
    return dict(
        outer_cos=f32(np.cos(outer)),
        outer_sin=f32(np.sin(outer)),
        inner_cos=f32(np.cos(inner)),
        inner_sin=f32(np.sin(inner)),
        twist_cos=f32(np.cos(twist)),
        twist_sin=f32(np.sin(twist)),
    )


def forward(first_re, first_im, t):
    tc = t["twist_cos"][:, None, :]
    ts = t["twist_sin"][:, None, :]
    b_re = first_re * tc + first_im * ts
    b_im = first_im * tc - first_re * ts
    dot = lambda a, m: jnp.einsum("krn,nm->krm", a, m, precision=HIGHEST)
    x_re = dot(b_re, t["inner_cos"]) + dot(b_im, t["inner_sin"])
    x_im = dot(b_im, t["inner_cos"]) - dot(b_re, t["inner_sin"])
    return x_re, x_im


def long_conv(signal, kernel):
    live, channels, cols = signal.shape
    rows = 2 * live
    t = tables(rows, cols)
    oc = t["outer_cos"][:, :live]
    os_ = t["outer_sin"][:, :live]
    sig = signal.astype(jnp.float32)
    s_re = jnp.einsum("kn,nrm->krm", oc, sig, precision=HIGHEST)
    s_im = -jnp.einsum("kn,nrm->krm", os_, sig, precision=HIGHEST)
    ker = kernel.reshape(channels, live, cols)
    h_re = jnp.einsum("kn,rnm->krm", oc, ker, precision=HIGHEST)
    h_im = -jnp.einsum("kn,rnm->krm", os_, ker, precision=HIGHEST)
    su_re, su_im = forward(s_re, s_im, t)
    sh_re, sh_im = forward(h_re, h_im, t)
    z_re = su_re * sh_re - su_im * sh_im
    z_im = su_re * sh_im + su_im * sh_re
    dot = lambda a, m: jnp.einsum("krn,nm->krm", a, m, precision=HIGHEST)
    d_re = dot(z_re, t["inner_cos"]) - dot(z_im, t["inner_sin"])
    d_im = dot(z_im, t["inner_cos"]) + dot(z_re, t["inner_sin"])
    tc = t["twist_cos"][:, None, :]
    ts = t["twist_sin"][:, None, :]
    e_re = d_re * tc - d_im * ts
    e_im = d_im * tc + d_re * ts
    scale = 1.0 / (rows * cols)
    back_cos = t["outer_cos"][:live] * scale
    back_sin = t["outer_sin"][:live] * scale
    return jnp.einsum("nk,krm->nrm", back_cos, e_re, precision=HIGHEST) - jnp.einsum(
        "nk,krm->nrm", back_sin, e_im, precision=HIGHEST
    )


def pick(values, axis, parity):
    shape = values.shape
    grouped = values.reshape(shape[:axis] + (shape[axis] // (2 * GROUP), 2, GROUP) + shape[axis + 1 :])
    taken = lax.dynamic_index_in_dim(grouped, parity, axis + 1, keepdims=False)
    return taken.reshape(shape[:axis] + (shape[axis] // 2,) + shape[axis + 1 :])


def on_device(tokens, w_proj, short_filter, long_filter, skip_gain):
    rows_dev = tokens.shape[0]
    margin = short_filter.shape[1] - 1
    width = w_proj.shape[2]
    half = width // 2
    chips = lax.axis_size("chip")
    parity = lax.axis_index("core")
    source = lax.all_gather(lax.all_gather(tokens, "mp", axis=1, tiled=True), "core", axis=0, tiled=True)
    split = w_proj.reshape(w_proj.shape[0], 3, width // (2 * GROUP), 2, GROUP)
    split = jnp.moveaxis(split, 3, 0).reshape(1, 2, w_proj.shape[0], 3, half)
    spread = jnp.broadcast_to(split, (chips, 2) + split.shape[2:]).reshape((2 * chips,) + split.shape[2:])
    weights = lax.all_to_all(spread, ("chip", "core"), split_axis=0, concat_axis=0, tiled=True)
    weights = weights.reshape(2 * chips * w_proj.shape[0], 3, half)
    projected = jnp.einsum(
        "td,dpc->tpc", source, weights, preferred_element_type=jnp.float32
    ).astype(jnp.bfloat16)
    rows = source.shape[0]
    tail = shifted(projected[rows - margin :], "chip", 1)
    extended = jnp.concatenate([tail, projected], axis=0).astype(jnp.float32)
    taps = pick(short_filter, 2, parity)
    mixed = jnp.zeros((rows, 3, half), jnp.float32)
    for offset in range(margin + 1):
        mixed = mixed + taps[:, offset, :][None] * extended[margin - offset : margin - offset + rows]
    query_rows = mixed[:, 0]
    product = (mixed[:, 1] * mixed[:, 2]).astype(jnp.bfloat16)
    outgoing = product.T.reshape(chips, GROUP, rows)
    arrived = lax.all_to_all(outgoing, "chip", split_axis=0, concat_axis=0, tiled=True)
    convolved = long_conv(arrived, long_filter).astype(jnp.bfloat16)
    returned = lax.all_to_all(convolved, "chip", split_axis=0, concat_axis=0, tiled=True)
    back_rows = returned.reshape(half, rows).T
    gain = pick(skip_gain, 0, parity)
    local = query_rows * (back_rows.astype(jnp.float32) + gain[None, :] * product.astype(jnp.float32))
    local = local.astype(jnp.bfloat16).reshape(2, rows_dev, half)
    swapped = lax.all_to_all(local, "core", split_axis=0, concat_axis=0, tiled=True)
    swapped = swapped.reshape(2, rows_dev, half // GROUP, GROUP)
    return jnp.transpose(swapped, (1, 2, 0, 3)).reshape(rows_dev, width)


def solution(mesh):
    seq_size = mesh.shape["seq"]
    devices = mesh.devices.reshape(seq_size // 2, 2, mesh.shape["mp"])
    inner = jax.sharding.Mesh(devices, ("chip", "core", "mp"))
    seq = ("chip", "core")
    return jax.shard_map(
        on_device,
        mesh=inner,
        in_specs=(
            P(seq, "mp"),
            P(seq, None, "mp"),
            P(None, None, "mp"),
            P(("mp",) + seq, None),
            P("mp"),
        ),
        out_specs=P(seq, "mp"),
        check_vma=False,
    )
```

```python
import numpy as np

import jax
import jax.numpy as jnp
from jax import lax
from jax.sharding import PartitionSpec as P

HIGHEST = lax.Precision.HIGHEST
GROUP = 8


def shifted(value, axis, steps):
    count = lax.axis_size(axis)
    leading, last = (max(0, -steps), min(count, count - steps))
    return lax.ppermute(value, axis, [(source, source + steps) for source in range(leading, last)])


def tables(rows, cols):
    first = np.arange(rows)
    second = np.arange(cols)
    outer = 2.0 * np.pi * np.outer(first, first) / rows
    inner = 2.0 * np.pi * np.outer(second, second) / cols
    twist = 2.0 * np.pi * np.outer(first, second) / (rows * cols)
    f32 = lambda a: jnp.asarray(a.astype(np.float32))
    return dict(
        outer_cos=f32(np.cos(outer)),
        outer_sin=f32(np.sin(outer)),
        inner_cos=f32(np.cos(inner)),
        inner_sin=f32(np.sin(inner)),
        twist_cos=f32(np.cos(twist)),
        twist_sin=f32(np.sin(twist)),
    )


def forward(first_re, first_im, t):
    tc = t["twist_cos"][:, None, :]
    ts = t["twist_sin"][:, None, :]
    b_re = first_re * tc + first_im * ts
    b_im = first_im * tc - first_re * ts
    dot = lambda a, m: jnp.einsum("krn,nm->krm", a, m, precision=HIGHEST)
    x_re = dot(b_re, t["inner_cos"]) + dot(b_im, t["inner_sin"])
    x_im = dot(b_im, t["inner_cos"]) - dot(b_re, t["inner_sin"])
    return x_re, x_im


def long_conv(signal, kernel):
    live, channels, cols = signal.shape
    rows = 2 * live
    t = tables(rows, cols)
    oc = t["outer_cos"][:, :live]
    os_ = t["outer_sin"][:, :live]
    sig = signal.astype(jnp.float32)
    s_re = jnp.einsum("kn,nrm->krm", oc, sig, precision=HIGHEST)
    s_im = -jnp.einsum("kn,nrm->krm", os_, sig, precision=HIGHEST)
    ker = kernel.reshape(channels, live, cols)
    h_re = jnp.einsum("kn,rnm->krm", oc, ker, precision=HIGHEST)
    h_im = -jnp.einsum("kn,rnm->krm", os_, ker, precision=HIGHEST)
    su_re, su_im = forward(s_re, s_im, t)
    sh_re, sh_im = forward(h_re, h_im, t)
    z_re = su_re * sh_re - su_im * sh_im
    z_im = su_re * sh_im + su_im * sh_re
    dot = lambda a, m: jnp.einsum("krn,nm->krm", a, m, precision=HIGHEST)
    d_re = dot(z_re, t["inner_cos"]) - dot(z_im, t["inner_sin"])
    d_im = dot(z_im, t["inner_cos"]) + dot(z_re, t["inner_sin"])
    tc = t["twist_cos"][:, None, :]
    ts = t["twist_sin"][:, None, :]
    e_re = d_re * tc - d_im * ts
    e_im = d_im * tc + d_re * ts
    scale = 1.0 / (rows * cols)
    back_cos = t["outer_cos"][:live] * scale
    back_sin = t["outer_sin"][:live] * scale
    return jnp.einsum("nk,krm->nrm", back_cos, e_re, precision=HIGHEST) - jnp.einsum(
        "nk,krm->nrm", back_sin, e_im, precision=HIGHEST
    )


def pick(values, axis, parity):
    shape = values.shape
    grouped = values.reshape(shape[:axis] + (shape[axis] // (2 * GROUP), 2, GROUP) + shape[axis + 1 :])
    taken = lax.dynamic_index_in_dim(grouped, parity, axis + 1, keepdims=False)
    return taken.reshape(shape[:axis] + (shape[axis] // 2,) + shape[axis + 1 :])


def on_device(tokens, w_proj, short_filter, long_filter, skip_gain):
    rows_dev = tokens.shape[0]
    margin = short_filter.shape[1] - 1
    width = w_proj.shape[2]
    half = width // 2
    chips = lax.axis_size("chip")
    parity = lax.axis_index("core")
    split = w_proj.reshape(w_proj.shape[0], 3, width // (2 * GROUP), 2, GROUP)
    weights = []
    for member in range(3):
        part = jnp.moveaxis(split[:, member], 2, 0).reshape(1, 2, w_proj.shape[0], half)
        spread = jnp.broadcast_to(part, (chips, 2) + part.shape[2:]).reshape((2 * chips,) + part.shape[2:])
        arrived = lax.all_to_all(spread, ("chip", "core"), split_axis=0, concat_axis=0, tiled=True)
        weights.append(arrived.reshape(2 * chips * w_proj.shape[0], half))
    source = lax.all_gather(lax.all_gather(tokens, "mp", axis=1, tiled=True), "core", axis=0, tiled=True)
    rows = source.shape[0]
    tail = shifted(source[rows - margin :], "chip", 1)
    extended_tokens = jnp.concatenate([tail, source], axis=0)
    taps = pick(short_filter, 2, parity)
    mixed = []
    for member in range(3):
        projected = jnp.dot(extended_tokens, weights[member], preferred_element_type=jnp.float32)
        extended = projected.astype(jnp.bfloat16).astype(jnp.float32)
        total = jnp.zeros((rows, half), jnp.float32)
        for offset in range(margin + 1):
            total = total + taps[member, offset][None] * extended[margin - offset : margin - offset + rows]
        mixed.append(total)
    query_rows = mixed[0]
    product = (mixed[1] * mixed[2]).astype(jnp.bfloat16)
    outgoing = product.T.reshape(chips, GROUP, rows)
    arrived = lax.all_to_all(outgoing, "chip", split_axis=0, concat_axis=0, tiled=True)
    convolved = long_conv(arrived, long_filter).astype(jnp.bfloat16)
    returned = lax.all_to_all(convolved, "chip", split_axis=0, concat_axis=0, tiled=True)
    back_rows = returned.reshape(half, rows).T
    gain = pick(skip_gain, 0, parity)
    local = query_rows * (back_rows.astype(jnp.float32) + gain[None, :] * product.astype(jnp.float32))
    local = local.astype(jnp.bfloat16).reshape(2, rows_dev, half)
    swapped = lax.all_to_all(local, "core", split_axis=0, concat_axis=0, tiled=True)
    swapped = swapped.reshape(2, rows_dev, half // GROUP, GROUP)
    return jnp.transpose(swapped, (1, 2, 0, 3)).reshape(rows_dev, width)


def solution(mesh):
    seq_size = mesh.shape["seq"]
    devices = mesh.devices.reshape(seq_size // 2, 2, mesh.shape["mp"])
    inner = jax.sharding.Mesh(devices, ("chip", "core", "mp"))
    seq = ("chip", "core")
    return jax.shard_map(
        on_device,
        mesh=inner,
        in_specs=(
            P(seq, "mp"),
            P(seq, None, "mp"),
            P(None, None, "mp"),
            P(("mp",) + seq, None),
            P("mp"),
        ),
        out_specs=P(seq, "mp"),
        check_vma=False,
    )
```

```python
import numpy as np

import jax
import jax.numpy as jnp
from jax import lax
from jax.sharding import PartitionSpec as P

HIGHEST = lax.Precision.HIGHEST
GROUP = 8


def shifted(value, axis, steps):
    count = lax.axis_size(axis)
    leading, last = (max(0, -steps), min(count, count - steps))
    return lax.ppermute(value, axis, [(source, source + steps) for source in range(leading, last)])


def tables(rows, cols):
    first = np.arange(rows)
    second = np.arange(cols)
    outer = 2.0 * np.pi * np.outer(first, first) / rows
    inner = 2.0 * np.pi * np.outer(second, second) / cols
    twist = 2.0 * np.pi * np.outer(first, second) / (rows * cols)
    f32 = lambda a: jnp.asarray(a.astype(np.float32))
    return dict(
        outer_cos=f32(np.cos(outer)),
        outer_sin=f32(np.sin(outer)),
        inner_cos=f32(np.cos(inner)),
        inner_sin=f32(np.sin(inner)),
        twist_cos=f32(np.cos(twist)),
        twist_sin=f32(np.sin(twist)),
    )


def forward(first_re, first_im, t):
    tc = t["twist_cos"][:, None, :]
    ts = t["twist_sin"][:, None, :]
    b_re = first_re * tc + first_im * ts
    b_im = first_im * tc - first_re * ts
    dot = lambda a, m: jnp.einsum("krn,nm->krm", a, m, precision=HIGHEST)
    x_re = dot(b_re, t["inner_cos"]) + dot(b_im, t["inner_sin"])
    x_im = dot(b_im, t["inner_cos"]) - dot(b_re, t["inner_sin"])
    return x_re, x_im


def long_conv(signal, kernel):
    live, channels, cols = signal.shape
    rows = 2 * live
    t = tables(rows, cols)
    oc = t["outer_cos"][:, :live]
    os_ = t["outer_sin"][:, :live]
    sig = signal.astype(jnp.float32)
    s_re = jnp.einsum("kn,nrm->krm", oc, sig, precision=HIGHEST)
    s_im = -jnp.einsum("kn,nrm->krm", os_, sig, precision=HIGHEST)
    ker = kernel.reshape(channels, live, cols)
    h_re = jnp.einsum("kn,rnm->krm", oc, ker, precision=HIGHEST)
    h_im = -jnp.einsum("kn,rnm->krm", os_, ker, precision=HIGHEST)
    su_re, su_im = forward(s_re, s_im, t)
    sh_re, sh_im = forward(h_re, h_im, t)
    z_re = su_re * sh_re - su_im * sh_im
    z_im = su_re * sh_im + su_im * sh_re
    dot = lambda a, m: jnp.einsum("krn,nm->krm", a, m, precision=HIGHEST)
    d_re = dot(z_re, t["inner_cos"]) - dot(z_im, t["inner_sin"])
    d_im = dot(z_im, t["inner_cos"]) + dot(z_re, t["inner_sin"])
    tc = t["twist_cos"][:, None, :]
    ts = t["twist_sin"][:, None, :]
    e_re = d_re * tc - d_im * ts
    e_im = d_im * tc + d_re * ts
    scale = 1.0 / (rows * cols)
    back_cos = t["outer_cos"][:live] * scale
    back_sin = t["outer_sin"][:live] * scale
    return jnp.einsum("nk,krm->nrm", back_cos, e_re, precision=HIGHEST) - jnp.einsum(
        "nk,krm->nrm", back_sin, e_im, precision=HIGHEST
    )


def pick(values, axis, parity):
    shape = values.shape
    grouped = values.reshape(shape[:axis] + (shape[axis] // (2 * GROUP), 2, GROUP) + shape[axis + 1 :])
    taken = lax.dynamic_index_in_dim(grouped, parity, axis + 1, keepdims=False)
    return taken.reshape(shape[:axis] + (shape[axis] // 2,) + shape[axis + 1 :])


def on_device(tokens, w_proj, short_filter, long_filter, skip_gain):
    rows_dev = tokens.shape[0]
    margin = short_filter.shape[1] - 1
    width = w_proj.shape[2]
    half = width // 2
    chips = lax.axis_size("chip")
    parity = lax.axis_index("core")
    split = w_proj.reshape(w_proj.shape[0], 3, width // (2 * GROUP), 2, GROUP)
    weights = [lax.all_gather(w_proj[:, 0], ("chip", "core"), axis=0, tiled=True)]
    for member in range(1, 3):
        part = jnp.moveaxis(split[:, member], 2, 0).reshape(1, 2, w_proj.shape[0], half)
        spread = jnp.broadcast_to(part, (chips, 2) + part.shape[2:]).reshape((2 * chips,) + part.shape[2:])
        arrived = lax.all_to_all(spread, ("chip", "core"), split_axis=0, concat_axis=0, tiled=True)
        weights.append(arrived.reshape(2 * chips * w_proj.shape[0], half))
    stacked = lax.all_gather(tokens, ("core", "mp"), axis=0, tiled=False)
    rows = 2 * rows_dev
    source = jnp.transpose(stacked.reshape(2, -1, rows_dev, tokens.shape[1]), (0, 2, 1, 3)).reshape(rows, -1)
    tail = shifted(source[rows - margin :], "chip", 1)
    extended_tokens = jnp.concatenate([tail, source], axis=0)
    taps = pick(short_filter, 2, parity)
    mixed = []
    for member in range(3):
        projected = jnp.dot(extended_tokens, weights[member], preferred_element_type=jnp.float32)
        if member == 0:
            projected = pick(projected, 1, parity)
        extended = projected.astype(jnp.bfloat16).astype(jnp.float32)
        total = jnp.zeros((rows, half), jnp.float32)
        for offset in range(margin + 1):
            total = total + taps[member, offset][None] * extended[margin - offset : margin - offset + rows]
        mixed.append(total)
    query_rows = mixed[0]
    product = (mixed[1] * mixed[2]).astype(jnp.bfloat16)
    outgoing = product.T.reshape(chips, GROUP, rows)
    arrived = lax.all_to_all(outgoing, "chip", split_axis=0, concat_axis=0, tiled=True)
    convolved = long_conv(arrived, long_filter).astype(jnp.bfloat16)
    returned = lax.all_to_all(convolved, "chip", split_axis=0, concat_axis=0, tiled=True)
    back_rows = returned.reshape(half, rows).T
    gain = pick(skip_gain, 0, parity)
    local = query_rows * (back_rows.astype(jnp.float32) + gain[None, :] * product.astype(jnp.float32))
    local = local.astype(jnp.bfloat16).reshape(2, rows_dev, half)
    swapped = lax.all_to_all(local, "core", split_axis=0, concat_axis=0, tiled=True)
    swapped = swapped.reshape(2, rows_dev, half // GROUP, GROUP)
    return jnp.transpose(swapped, (1, 2, 0, 3)).reshape(rows_dev, width)


def solution(mesh):
    seq_size = mesh.shape["seq"]
    devices = mesh.devices.reshape(seq_size // 2, 2, mesh.shape["mp"])
    inner = jax.sharding.Mesh(devices, ("chip", "core", "mp"))
    seq = ("chip", "core")
    return jax.shard_map(
        on_device,
        mesh=inner,
        in_specs=(
            P(seq, "mp"),
            P(seq, None, "mp"),
            P(None, None, "mp"),
            P(("mp",) + seq, None),
            P("mp"),
        ),
        out_specs=P(seq, "mp"),
        check_vma=False,
    )
```

```python
import numpy as np

import jax
import jax.numpy as jnp
from jax import lax
from jax.sharding import PartitionSpec as P

HIGHEST = lax.Precision.HIGHEST
GROUP = 8


def shifted(value, axis, steps):
    count = lax.axis_size(axis)
    leading, last = (max(0, -steps), min(count, count - steps))
    return lax.ppermute(value, axis, [(source, source + steps) for source in range(leading, last)])


def tables(rows, cols):
    first = np.arange(rows)
    second = np.arange(cols)
    outer = 2.0 * np.pi * np.outer(first, first) / rows
    inner = 2.0 * np.pi * np.outer(second, second) / cols
    twist = 2.0 * np.pi * np.outer(first, second) / (rows * cols)
    f32 = lambda a: jnp.asarray(a.astype(np.float32))
    return dict(
        outer_cos=f32(np.cos(outer)),
        outer_sin=f32(np.sin(outer)),
        inner_cos=f32(np.cos(inner)),
        inner_sin=f32(np.sin(inner)),
        twist_cos=f32(np.cos(twist)),
        twist_sin=f32(np.sin(twist)),
    )


def forward(first_re, first_im, t):
    tc = t["twist_cos"][:, None, :]
    ts = t["twist_sin"][:, None, :]
    b_re = first_re * tc + first_im * ts
    b_im = first_im * tc - first_re * ts
    dot = lambda a, m: jnp.einsum("krn,nm->krm", a, m, precision=HIGHEST)
    x_re = dot(b_re, t["inner_cos"]) + dot(b_im, t["inner_sin"])
    x_im = dot(b_im, t["inner_cos"]) - dot(b_re, t["inner_sin"])
    return x_re, x_im


def long_conv(signal, kernel):
    live, channels, cols = signal.shape
    rows = 2 * live
    t = tables(rows, cols)
    oc = t["outer_cos"][:, :live]
    os_ = t["outer_sin"][:, :live]
    sig = signal.astype(jnp.float32)
    s_re = jnp.einsum("kn,nrm->krm", oc, sig, precision=HIGHEST)
    s_im = -jnp.einsum("kn,nrm->krm", os_, sig, precision=HIGHEST)
    ker = kernel.reshape(channels, live, cols)
    h_re = jnp.einsum("kn,rnm->krm", oc, ker, precision=HIGHEST)
    h_im = -jnp.einsum("kn,rnm->krm", os_, ker, precision=HIGHEST)
    su_re, su_im = forward(s_re, s_im, t)
    sh_re, sh_im = forward(h_re, h_im, t)
    z_re = su_re * sh_re - su_im * sh_im
    z_im = su_re * sh_im + su_im * sh_re
    dot = lambda a, m: jnp.einsum("krn,nm->krm", a, m, precision=HIGHEST)
    d_re = dot(z_re, t["inner_cos"]) - dot(z_im, t["inner_sin"])
    d_im = dot(z_im, t["inner_cos"]) + dot(z_re, t["inner_sin"])
    tc = t["twist_cos"][:, None, :]
    ts = t["twist_sin"][:, None, :]
    e_re = d_re * tc - d_im * ts
    e_im = d_im * tc + d_re * ts
    scale = 1.0 / (rows * cols)
    back_cos = t["outer_cos"][:live] * scale
    back_sin = t["outer_sin"][:live] * scale
    return jnp.einsum("nk,krm->nrm", back_cos, e_re, precision=HIGHEST) - jnp.einsum(
        "nk,krm->nrm", back_sin, e_im, precision=HIGHEST
    )


def pick(values, axis, parity):
    shape = values.shape
    grouped = values.reshape(shape[:axis] + (shape[axis] // (2 * GROUP), 2, GROUP) + shape[axis + 1 :])
    taken = lax.dynamic_index_in_dim(grouped, parity, axis + 1, keepdims=False)
    return taken.reshape(shape[:axis] + (shape[axis] // 2,) + shape[axis + 1 :])


def on_device(tokens, w_proj, short_filter, long_filter, skip_gain):
    rows_dev = tokens.shape[0]
    margin = short_filter.shape[1] - 1
    width = w_proj.shape[2]
    half = width // 2
    chips = lax.axis_size("chip")
    parity = lax.axis_index("core")
    split = w_proj.reshape(w_proj.shape[0], 3, width // (2 * GROUP), 2, GROUP)
    split = jnp.transpose(split, (1, 3, 0, 2, 4)).reshape(3, 1, 2, w_proj.shape[0], half)
    spread = jnp.broadcast_to(split, (3, chips, 2) + split.shape[3:]).reshape((3, 2 * chips) + split.shape[3:])
    arrived = lax.all_to_all(spread, ("chip", "core"), split_axis=1, concat_axis=1, tiled=True)
    weights = arrived.reshape(3, 2 * chips * w_proj.shape[0], half)
    stacked = lax.all_gather(tokens, ("core", "mp"), axis=0, tiled=False)
    rows = 2 * rows_dev
    source = jnp.transpose(stacked.reshape(2, -1, rows_dev, tokens.shape[1]), (0, 2, 1, 3)).reshape(rows, -1)
    tail = shifted(source[rows - margin :], "chip", 1)
    extended_tokens = jnp.concatenate([tail, source], axis=0)
    taps = pick(short_filter, 2, parity)
    mixed = []
    for member in range(3):
        projected = jnp.dot(extended_tokens, weights[member], preferred_element_type=jnp.float32)
        extended = projected.astype(jnp.bfloat16).astype(jnp.float32)
        total = jnp.zeros((rows, half), jnp.float32)
        for offset in range(margin + 1):
            total = total + taps[member, offset][None] * extended[margin - offset : margin - offset + rows]
        mixed.append(total)
    query_rows = mixed[0]
    product = (mixed[1] * mixed[2]).astype(jnp.bfloat16)
    outgoing = product.T.reshape(chips, GROUP, rows)
    arrived = lax.all_to_all(outgoing, "chip", split_axis=0, concat_axis=0, tiled=True)
    convolved = long_conv(arrived, long_filter).astype(jnp.bfloat16)
    returned = lax.all_to_all(convolved, "chip", split_axis=0, concat_axis=0, tiled=True)
    back_rows = returned.reshape(half, rows).T
    gain = pick(skip_gain, 0, parity)
    local = query_rows * (back_rows.astype(jnp.float32) + gain[None, :] * product.astype(jnp.float32))
    local = local.astype(jnp.bfloat16).reshape(2, rows_dev, half)
    swapped = lax.all_to_all(local, "core", split_axis=0, concat_axis=0, tiled=True)
    swapped = swapped.reshape(2, rows_dev, half // GROUP, GROUP)
    return jnp.transpose(swapped, (1, 2, 0, 3)).reshape(rows_dev, width)


def solution(mesh):
    seq_size = mesh.shape["seq"]
    devices = mesh.devices.reshape(seq_size // 2, 2, mesh.shape["mp"])
    inner = jax.sharding.Mesh(devices, ("chip", "core", "mp"))
    seq = ("chip", "core")
    return jax.shard_map(
        on_device,
        mesh=inner,
        in_specs=(
            P(seq, "mp"),
            P(seq, None, "mp"),
            P(None, None, "mp"),
            P(("mp",) + seq, None),
            P("mp"),
        ),
        out_specs=P(seq, "mp"),
        check_vma=False,
    )
```

```python
import numpy as np

import jax
import jax.numpy as jnp
from jax import lax
from jax.sharding import PartitionSpec as P

HIGHEST = lax.Precision.HIGHEST
GROUP = 8


def shifted(value, axis, steps):
    count = lax.axis_size(axis)
    leading, last = (max(0, -steps), min(count, count - steps))
    return lax.ppermute(value, axis, [(source, source + steps) for source in range(leading, last)])


def tables(rows, cols):
    first = np.arange(rows)
    second = np.arange(cols)
    outer = 2.0 * np.pi * np.outer(first, first) / rows
    inner = 2.0 * np.pi * np.outer(second, second) / cols
    twist = 2.0 * np.pi * np.outer(first, second) / (rows * cols)
    f32 = lambda a: jnp.asarray(a.astype(np.float32))
    return dict(
        outer_cos=f32(np.cos(outer)),
        outer_sin=f32(np.sin(outer)),
        inner_cos=f32(np.cos(inner)),
        inner_sin=f32(np.sin(inner)),
        twist_cos=f32(np.cos(twist)),
        twist_sin=f32(np.sin(twist)),
    )


def forward(first_re, first_im, t):
    tc = t["twist_cos"][:, None, :]
    ts = t["twist_sin"][:, None, :]
    b_re = first_re * tc + first_im * ts
    b_im = first_im * tc - first_re * ts
    dot = lambda a, m: jnp.einsum("krn,nm->krm", a, m, precision=HIGHEST)
    x_re = dot(b_re, t["inner_cos"]) + dot(b_im, t["inner_sin"])
    x_im = dot(b_im, t["inner_cos"]) - dot(b_re, t["inner_sin"])
    return x_re, x_im


def long_conv(signal, kernel):
    live, channels, cols = signal.shape
    rows = 2 * live
    t = tables(rows, cols)
    oc = t["outer_cos"][:, :live]
    os_ = t["outer_sin"][:, :live]
    sig = signal.astype(jnp.float32)
    s_re = jnp.einsum("kn,nrm->krm", oc, sig, precision=HIGHEST)
    s_im = -jnp.einsum("kn,nrm->krm", os_, sig, precision=HIGHEST)
    ker = kernel.reshape(channels, live, cols)
    h_re = jnp.einsum("kn,rnm->krm", oc, ker, precision=HIGHEST)
    h_im = -jnp.einsum("kn,rnm->krm", os_, ker, precision=HIGHEST)
    su_re, su_im = forward(s_re, s_im, t)
    sh_re, sh_im = forward(h_re, h_im, t)
    z_re = su_re * sh_re - su_im * sh_im
    z_im = su_re * sh_im + su_im * sh_re
    dot = lambda a, m: jnp.einsum("krn,nm->krm", a, m, precision=HIGHEST)
    d_re = dot(z_re, t["inner_cos"]) - dot(z_im, t["inner_sin"])
    d_im = dot(z_im, t["inner_cos"]) + dot(z_re, t["inner_sin"])
    tc = t["twist_cos"][:, None, :]
    ts = t["twist_sin"][:, None, :]
    e_re = d_re * tc - d_im * ts
    e_im = d_im * tc + d_re * ts
    scale = 1.0 / (rows * cols)
    back_cos = t["outer_cos"][:live] * scale
    back_sin = t["outer_sin"][:live] * scale
    return jnp.einsum("nk,krm->nrm", back_cos, e_re, precision=HIGHEST) - jnp.einsum(
        "nk,krm->nrm", back_sin, e_im, precision=HIGHEST
    )


def pick(values, axis, parity):
    shape = values.shape
    grouped = values.reshape(shape[:axis] + (shape[axis] // (2 * GROUP), 2, GROUP) + shape[axis + 1 :])
    taken = lax.dynamic_index_in_dim(grouped, parity, axis + 1, keepdims=False)
    return taken.reshape(shape[:axis] + (shape[axis] // 2,) + shape[axis + 1 :])


def on_device(tokens, w_proj, short_filter, long_filter, skip_gain):
    rows_dev = tokens.shape[0]
    margin = short_filter.shape[1] - 1
    width = w_proj.shape[2]
    half = width // 2
    chips = lax.axis_size("chip")
    parity = lax.axis_index("core")
    split = w_proj.reshape(w_proj.shape[0], 3, width // (2 * GROUP), 2, GROUP)
    split = jnp.transpose(split, (3, 0, 1, 2, 4)).reshape(1, 2, w_proj.shape[0], 3 * half)
    spread = jnp.broadcast_to(split, (chips,) + split.shape[1:]).reshape((2 * chips,) + split.shape[2:])
    arrived = lax.all_to_all(spread, ("chip", "core"), split_axis=0, concat_axis=0, tiled=True)
    weights = arrived.reshape(2 * chips * w_proj.shape[0], 3 * half)
    stacked = lax.all_gather(tokens, ("core", "mp"), axis=0, tiled=False)
    rows = 2 * rows_dev
    source = jnp.transpose(stacked.reshape(2, -1, rows_dev, tokens.shape[1]), (0, 2, 1, 3)).reshape(rows, -1)
    tail = shifted(source[rows - margin :], "chip", 1)
    extended_tokens = jnp.concatenate([tail, source], axis=0)
    taps = pick(short_filter, 2, parity)
    mixed = []
    projected_all = jnp.dot(extended_tokens, weights, preferred_element_type=jnp.float32)
    for member in range(3):
        projected = projected_all[:, member * half : (member + 1) * half]
        extended = projected.astype(jnp.bfloat16).astype(jnp.float32)
        total = jnp.zeros((rows, half), jnp.float32)
        for offset in range(margin + 1):
            total = total + taps[member, offset][None] * extended[margin - offset : margin - offset + rows]
        mixed.append(total)
    query_rows = mixed[0]
    product = (mixed[1] * mixed[2]).astype(jnp.bfloat16)
    outgoing = product.T.reshape(chips, GROUP, rows)
    arrived = lax.all_to_all(outgoing, "chip", split_axis=0, concat_axis=0, tiled=True)
    convolved = long_conv(arrived, long_filter).astype(jnp.bfloat16)
    returned = lax.all_to_all(convolved, "chip", split_axis=0, concat_axis=0, tiled=True)
    back_rows = returned.reshape(half, rows).T
    gain = pick(skip_gain, 0, parity)
    local = query_rows * (back_rows.astype(jnp.float32) + gain[None, :] * product.astype(jnp.float32))
    local = local.astype(jnp.bfloat16).reshape(2, rows_dev, half)
    swapped = lax.all_to_all(local, "core", split_axis=0, concat_axis=0, tiled=True)
    swapped = swapped.reshape(2, rows_dev, half // GROUP, GROUP)
    return jnp.transpose(swapped, (1, 2, 0, 3)).reshape(rows_dev, width)


def solution(mesh):
    seq_size = mesh.shape["seq"]
    devices = mesh.devices.reshape(seq_size // 2, 2, mesh.shape["mp"])
    inner = jax.sharding.Mesh(devices, ("chip", "core", "mp"))
    seq = ("chip", "core")
    return jax.shard_map(
        on_device,
        mesh=inner,
        in_specs=(
            P(seq, "mp"),
            P(seq, None, "mp"),
            P(None, None, "mp"),
            P(("mp",) + seq, None),
            P("mp"),
        ),
        out_specs=P(seq, "mp"),
        check_vma=False,
    )
```

```python
import numpy as np

import jax
import jax.numpy as jnp
from jax import lax
from jax.sharding import PartitionSpec as P

HIGHEST = lax.Precision.HIGHEST
GROUP = 8


def shifted(value, axis, steps):
    count = lax.axis_size(axis)
    leading, last = (max(0, -steps), min(count, count - steps))
    return lax.ppermute(value, axis, [(source, source + steps) for source in range(leading, last)])


def tables(rows, cols):
    first = np.arange(rows)
    second = np.arange(cols)
    outer = 2.0 * np.pi * np.outer(first, first) / rows
    inner = 2.0 * np.pi * np.outer(second, second) / cols
    twist = 2.0 * np.pi * np.outer(first, second) / (rows * cols)
    f32 = lambda a: jnp.asarray(a.astype(np.float32))
    return dict(
        outer_cos=f32(np.cos(outer)),
        outer_sin=f32(np.sin(outer)),
        inner_cos=f32(np.cos(inner)),
        inner_sin=f32(np.sin(inner)),
        twist_cos=f32(np.cos(twist)),
        twist_sin=f32(np.sin(twist)),
    )


def forward(first_re, first_im, t):
    tc = t["twist_cos"][:, None, :]
    ts = t["twist_sin"][:, None, :]
    b_re = first_re * tc + first_im * ts
    b_im = first_im * tc - first_re * ts
    dot = lambda a, m: jnp.einsum("krn,nm->krm", a, m, precision=HIGHEST)
    x_re = dot(b_re, t["inner_cos"]) + dot(b_im, t["inner_sin"])
    x_im = dot(b_im, t["inner_cos"]) - dot(b_re, t["inner_sin"])
    return x_re, x_im


def long_conv(signal, kernel):
    live, channels, cols = signal.shape
    rows = 2 * live
    t = tables(rows, cols)
    oc = t["outer_cos"][:, :live]
    os_ = t["outer_sin"][:, :live]
    sig = signal.astype(jnp.float32)
    s_re = jnp.einsum("kn,nrm->krm", oc, sig, precision=HIGHEST)
    s_im = -jnp.einsum("kn,nrm->krm", os_, sig, precision=HIGHEST)
    ker = kernel.reshape(channels, live, cols)
    h_re = jnp.einsum("kn,rnm->krm", oc, ker, precision=HIGHEST)
    h_im = -jnp.einsum("kn,rnm->krm", os_, ker, precision=HIGHEST)
    su_re, su_im = forward(s_re, s_im, t)
    sh_re, sh_im = forward(h_re, h_im, t)
    z_re = su_re * sh_re - su_im * sh_im
    z_im = su_re * sh_im + su_im * sh_re
    dot = lambda a, m: jnp.einsum("krn,nm->krm", a, m, precision=HIGHEST)
    d_re = dot(z_re, t["inner_cos"]) - dot(z_im, t["inner_sin"])
    d_im = dot(z_im, t["inner_cos"]) + dot(z_re, t["inner_sin"])
    tc = t["twist_cos"][:, None, :]
    ts = t["twist_sin"][:, None, :]
    e_re = d_re * tc - d_im * ts
    e_im = d_im * tc + d_re * ts
    scale = 1.0 / (rows * cols)
    back_cos = t["outer_cos"][:live] * scale
    back_sin = t["outer_sin"][:live] * scale
    return jnp.einsum("nk,krm->nrm", back_cos, e_re, precision=HIGHEST) - jnp.einsum(
        "nk,krm->nrm", back_sin, e_im, precision=HIGHEST
    )


def pick(values, axis, parity):
    shape = values.shape
    grouped = values.reshape(shape[:axis] + (shape[axis] // (2 * GROUP), 2, GROUP) + shape[axis + 1 :])
    taken = lax.dynamic_index_in_dim(grouped, parity, axis + 1, keepdims=False)
    return taken.reshape(shape[:axis] + (shape[axis] // 2,) + shape[axis + 1 :])


CHIP = ("xh", "xl", "zl", "y")
HALF = ("xl", "zl", "y", "core")


def swap(value, axis):
    return lax.ppermute(value, axis, [(0, 1), (1, 0)])


def on_device(tokens, w_proj, short_filter, long_filter, skip_gain):
    rows_dev = tokens.shape[0]
    margin = short_filter.shape[1] - 1
    width = w_proj.shape[2]
    half = width // 2
    chips = lax.axis_size(CHIP)
    senders = lax.axis_size(HALF)
    parity = lax.axis_index("core")
    side = lax.axis_index("xh")
    split = w_proj.reshape(w_proj.shape[0], 3, width // (2 * GROUP), 2, GROUP)
    split = jnp.transpose(split, (3, 0, 1, 2, 4)).reshape(1, 2, w_proj.shape[0], 3 * half)
    spread = jnp.broadcast_to(split, (senders // 2,) + split.shape[1:]).reshape((senders,) + split.shape[2:])
    arrived = lax.all_to_all(spread, HALF, split_axis=0, concat_axis=0, tiled=True)
    weights = arrived.reshape(senders * w_proj.shape[0], 3 * half)
    depth = weights.shape[0]
    stacked = lax.all_gather(tokens, ("core", "mp"), axis=0, tiled=False)
    rows = 2 * rows_dev
    source = jnp.transpose(stacked.reshape(2, -1, rows_dev, tokens.shape[1]), (0, 2, 1, 3)).reshape(rows, -1)
    tail = shifted(source[rows - margin :], CHIP, 1)
    extended_tokens = jnp.concatenate([tail, source], axis=0)
    mine = lax.dynamic_slice_in_dim(extended_tokens, side * depth, depth, axis=1)
    other = lax.dynamic_slice_in_dim(extended_tokens, (1 - side) * depth, depth, axis=1)
    theirs = swap(other, "xh")
    own_part = jnp.dot(mine, weights, preferred_element_type=jnp.float32)
    their_part = jnp.dot(theirs, weights, preferred_element_type=jnp.float32)
    projected_all = own_part + swap(their_part, "xh")
    taps = pick(short_filter, 2, parity)
    mixed = []
    for member in range(3):
        projected = projected_all[:, member * half : (member + 1) * half]
        extended = projected.astype(jnp.bfloat16).astype(jnp.float32)
        total = jnp.zeros((rows, half), jnp.float32)
        for offset in range(margin + 1):
            total = total + taps[member, offset][None] * extended[margin - offset : margin - offset + rows]
        mixed.append(total)
    query_rows = mixed[0]
    product = (mixed[1] * mixed[2]).astype(jnp.bfloat16)
    outgoing = product.T.reshape(chips, GROUP, rows)
    arrived = lax.all_to_all(outgoing, CHIP, split_axis=0, concat_axis=0, tiled=True)
    convolved = long_conv(arrived, long_filter).astype(jnp.bfloat16)
    returned = lax.all_to_all(convolved, CHIP, split_axis=0, concat_axis=0, tiled=True)
    back_rows = returned.reshape(half, rows).T
    gain = pick(skip_gain, 0, parity)
    local = query_rows * (back_rows.astype(jnp.float32) + gain[None, :] * product.astype(jnp.float32))
    local = local.astype(jnp.bfloat16).reshape(2, rows_dev, half)
    swapped = lax.all_to_all(local, "core", split_axis=0, concat_axis=0, tiled=True)
    swapped = swapped.reshape(2, rows_dev, half // GROUP, GROUP)
    return jnp.transpose(swapped, (1, 2, 0, 3)).reshape(rows_dev, width)


def solution(mesh):
    physical = (2, 2, 2, 4, 2)
    devices = mesh.devices.reshape(physical + (mesh.shape["mp"],))
    inner = jax.sharding.Mesh(devices, CHIP + ("core", "mp"))
    seq = CHIP + ("core",)
    return jax.shard_map(
        on_device,
        mesh=inner,
        in_specs=(
            P(seq, "mp"),
            P(seq, None, "mp"),
            P(None, None, "mp"),
            P(("mp",) + seq, None),
            P("mp"),
        ),
        out_specs=P(seq, "mp"),
        check_vma=False,
    )
```

```python
import numpy as np

import jax
import jax.numpy as jnp
from jax import lax
from jax.sharding import PartitionSpec as P

HIGHEST = lax.Precision.HIGHEST
GROUP = 8


def shifted(value, axis, steps):
    count = lax.axis_size(axis)
    leading, last = (max(0, -steps), min(count, count - steps))
    return lax.ppermute(value, axis, [(source, source + steps) for source in range(leading, last)])


def tables(rows, cols):
    first = np.arange(rows)
    second = np.arange(cols)
    outer = 2.0 * np.pi * np.outer(first, first) / rows
    inner = 2.0 * np.pi * np.outer(second, second) / cols
    twist = 2.0 * np.pi * np.outer(first, second) / (rows * cols)
    f32 = lambda a: jnp.asarray(a.astype(np.float32))
    return dict(
        outer_cos=f32(np.cos(outer)),
        outer_sin=f32(np.sin(outer)),
        inner_cos=f32(np.cos(inner)),
        inner_sin=f32(np.sin(inner)),
        twist_cos=f32(np.cos(twist)),
        twist_sin=f32(np.sin(twist)),
    )


def forward(first_re, first_im, t):
    tc = t["twist_cos"][:, None, :]
    ts = t["twist_sin"][:, None, :]
    b_re = first_re * tc + first_im * ts
    b_im = first_im * tc - first_re * ts
    dot = lambda a, m: jnp.einsum("krn,nm->krm", a, m, precision=HIGHEST)
    x_re = dot(b_re, t["inner_cos"]) + dot(b_im, t["inner_sin"])
    x_im = dot(b_im, t["inner_cos"]) - dot(b_re, t["inner_sin"])
    return x_re, x_im


def long_conv(signal, kernel):
    live, channels, cols = signal.shape
    rows = 2 * live
    t = tables(rows, cols)
    oc = t["outer_cos"][:, :live]
    os_ = t["outer_sin"][:, :live]
    sig = signal.astype(jnp.float32)
    s_re = jnp.einsum("kn,nrm->krm", oc, sig, precision=HIGHEST)
    s_im = -jnp.einsum("kn,nrm->krm", os_, sig, precision=HIGHEST)
    ker = kernel.reshape(channels, live, cols)
    h_re = jnp.einsum("kn,rnm->krm", oc, ker, precision=HIGHEST)
    h_im = -jnp.einsum("kn,rnm->krm", os_, ker, precision=HIGHEST)
    su_re, su_im = forward(s_re, s_im, t)
    sh_re, sh_im = forward(h_re, h_im, t)
    z_re = su_re * sh_re - su_im * sh_im
    z_im = su_re * sh_im + su_im * sh_re
    dot = lambda a, m: jnp.einsum("krn,nm->krm", a, m, precision=HIGHEST)
    d_re = dot(z_re, t["inner_cos"]) - dot(z_im, t["inner_sin"])
    d_im = dot(z_im, t["inner_cos"]) + dot(z_re, t["inner_sin"])
    tc = t["twist_cos"][:, None, :]
    ts = t["twist_sin"][:, None, :]
    e_re = d_re * tc - d_im * ts
    e_im = d_im * tc + d_re * ts
    scale = 1.0 / (rows * cols)
    back_cos = t["outer_cos"][:live] * scale
    back_sin = t["outer_sin"][:live] * scale
    return jnp.einsum("nk,krm->nrm", back_cos, e_re, precision=HIGHEST) - jnp.einsum(
        "nk,krm->nrm", back_sin, e_im, precision=HIGHEST
    )


def pick(values, axis, parity):
    shape = values.shape
    grouped = values.reshape(shape[:axis] + (shape[axis] // (2 * GROUP), 2, GROUP) + shape[axis + 1 :])
    taken = lax.dynamic_index_in_dim(grouped, parity, axis + 1, keepdims=False)
    return taken.reshape(shape[:axis] + (shape[axis] // 2,) + shape[axis + 1 :])


CHIP = ("xh", "xl", "zl", "y")
HALF = ("xl", "zl", "y", "core")


def swap(value, axis):
    return lax.ppermute(value, axis, [(0, 1), (1, 0)])


def on_device(tokens, w_proj, short_filter, long_filter, skip_gain):
    rows_dev = tokens.shape[0]
    margin = short_filter.shape[1] - 1
    width = w_proj.shape[2]
    half = width // 2
    chips = lax.axis_size(CHIP)
    senders = lax.axis_size(HALF)
    parity = lax.axis_index("core")
    side = lax.axis_index("xh")
    split = w_proj.reshape(w_proj.shape[0], 3, width // (2 * GROUP), 2, GROUP)
    split = jnp.transpose(split, (3, 0, 1, 2, 4)).reshape(1, 2, w_proj.shape[0], 3 * half)
    spread = jnp.broadcast_to(split, (senders // 2,) + split.shape[1:]).reshape((senders,) + split.shape[2:])
    arrived = lax.all_to_all(spread, HALF, split_axis=0, concat_axis=0, tiled=True)
    weights = arrived.reshape(senders * w_proj.shape[0], 3 * half)
    depth = weights.shape[0]
    stacked = lax.all_gather(tokens, ("xh", "core", "mp"), axis=0, tiled=False)
    rows = 2 * rows_dev
    stacked = stacked.reshape(2, 2, -1, rows_dev, tokens.shape[1])
    both = jnp.transpose(stacked, (0, 1, 3, 2, 4)).reshape(2, rows, -1)
    mine = lax.dynamic_slice_in_dim(both, side * depth, depth, axis=2)
    own_part = jnp.dot(lax.dynamic_index_in_dim(mine, side, 0, keepdims=False), weights,
                       preferred_element_type=jnp.float32)
    their_part = jnp.dot(lax.dynamic_index_in_dim(mine, 1 - side, 0, keepdims=False), weights,
                         preferred_element_type=jnp.float32)
    summed = (own_part + swap(their_part, "xh")).astype(jnp.bfloat16)
    tail = shifted(summed[rows - margin :], CHIP, 1)
    projected_all = jnp.concatenate([tail, summed], axis=0).astype(jnp.float32)
    taps = pick(short_filter, 2, parity)
    mixed = []
    for member in range(3):
        extended = projected_all[:, member * half : (member + 1) * half]
        total = jnp.zeros((rows, half), jnp.float32)
        for offset in range(margin + 1):
            total = total + taps[member, offset][None] * extended[margin - offset : margin - offset + rows]
        mixed.append(total)
    query_rows = mixed[0]
    product = (mixed[1] * mixed[2]).astype(jnp.bfloat16)
    outgoing = product.T.reshape(chips, GROUP, rows)
    arrived = lax.all_to_all(outgoing, CHIP, split_axis=0, concat_axis=0, tiled=True)
    convolved = long_conv(arrived, long_filter).astype(jnp.bfloat16)
    returned = lax.all_to_all(convolved, CHIP, split_axis=0, concat_axis=0, tiled=True)
    back_rows = returned.reshape(half, rows).T
    gain = pick(skip_gain, 0, parity)
    local = query_rows * (back_rows.astype(jnp.float32) + gain[None, :] * product.astype(jnp.float32))
    local = local.astype(jnp.bfloat16).reshape(2, rows_dev, half)
    swapped = lax.all_to_all(local, "core", split_axis=0, concat_axis=0, tiled=True)
    swapped = swapped.reshape(2, rows_dev, half // GROUP, GROUP)
    return jnp.transpose(swapped, (1, 2, 0, 3)).reshape(rows_dev, width)


def solution(mesh):
    physical = (2, 2, 2, 4, 2)
    devices = mesh.devices.reshape(physical + (mesh.shape["mp"],))
    inner = jax.sharding.Mesh(devices, CHIP + ("core", "mp"))
    seq = CHIP + ("core",)
    return jax.shard_map(
        on_device,
        mesh=inner,
        in_specs=(
            P(seq, "mp"),
            P(seq, None, "mp"),
            P(None, None, "mp"),
            P(("mp",) + seq, None),
            P("mp"),
        ),
        out_specs=P(seq, "mp"),
        check_vma=False,
    )
```

```python
import numpy as np

import jax
import jax.numpy as jnp
from jax import lax
from jax.sharding import PartitionSpec as P

HIGHEST = lax.Precision.HIGHEST
GROUP = 8


def shifted(value, axis, steps):
    count = lax.axis_size(axis)
    leading, last = (max(0, -steps), min(count, count - steps))
    return lax.ppermute(value, axis, [(source, source + steps) for source in range(leading, last)])


def tables(rows, cols):
    first = np.arange(rows)
    second = np.arange(cols)
    outer = 2.0 * np.pi * np.outer(first, first) / rows
    inner = 2.0 * np.pi * np.outer(second, second) / cols
    twist = 2.0 * np.pi * np.outer(first, second) / (rows * cols)
    f32 = lambda a: jnp.asarray(a.astype(np.float32))
    return dict(
        outer_cos=f32(np.cos(outer)),
        outer_sin=f32(np.sin(outer)),
        inner_cos=f32(np.cos(inner)),
        inner_sin=f32(np.sin(inner)),
        twist_cos=f32(np.cos(twist)),
        twist_sin=f32(np.sin(twist)),
    )


def block(cos, sin, sign):
    return jnp.concatenate(
        [jnp.concatenate([cos, sign * sin], axis=1), jnp.concatenate([-sign * sin, cos], axis=1)], axis=0
    )


def forward(first, t, cols):
    tc = t["twist_cos"][:, None, :]
    ts = t["twist_sin"][:, None, :]
    first_re, first_im = first[..., :cols], first[..., cols:]
    turned = jnp.concatenate([first_re * tc + first_im * ts, first_im * tc - first_re * ts], axis=-1)
    return jnp.einsum("krn,nm->krm", turned, block(t["inner_cos"], t["inner_sin"], -1.0), precision=HIGHEST)


def long_conv(signal, kernel):
    live, channels, cols = signal.shape
    rows = 2 * live
    t = lax.optimization_barrier(tables(rows, cols))
    first = jnp.concatenate([t["outer_cos"][:, :live], -t["outer_sin"][:, :live]], axis=0)
    sig = jnp.einsum("kn,nrm->krm", first, signal.astype(jnp.float32), precision=HIGHEST)
    ker = jnp.einsum("kn,rnm->krm", first, kernel.reshape(channels, live, cols), precision=HIGHEST)
    sig = jnp.concatenate([sig[:rows], sig[rows:]], axis=-1)
    ker = jnp.concatenate([ker[:rows], ker[rows:]], axis=-1)
    su = forward(sig, t, cols)
    sh = forward(ker, t, cols)
    su_re, su_im = su[..., :cols], su[..., cols:]
    sh_re, sh_im = sh[..., :cols], sh[..., cols:]
    z = jnp.concatenate([su_re * sh_re - su_im * sh_im, su_re * sh_im + su_im * sh_re], axis=-1)
    d = jnp.einsum("krn,nm->krm", z, block(t["inner_cos"], t["inner_sin"], 1.0), precision=HIGHEST)
    d_re, d_im = d[..., :cols], d[..., cols:]
    tc = t["twist_cos"][:, None, :]
    ts = t["twist_sin"][:, None, :]
    e = jnp.concatenate([d_re * tc - d_im * ts, d_im * tc + d_re * ts], axis=0)
    scale = 1.0 / (rows * cols)
    back = jnp.concatenate([t["outer_cos"][:live], -t["outer_sin"][:live]], axis=1) * scale
    return jnp.einsum("nk,krm->nrm", back, e, precision=HIGHEST)


def pick(values, axis, parity):
    shape = values.shape
    grouped = values.reshape(shape[:axis] + (shape[axis] // (2 * GROUP), 2, GROUP) + shape[axis + 1 :])
    taken = lax.dynamic_index_in_dim(grouped, parity, axis + 1, keepdims=False)
    return taken.reshape(shape[:axis] + (shape[axis] // 2,) + shape[axis + 1 :])


def on_device(tokens, w_proj, short_filter, long_filter, skip_gain):
    rows_dev = tokens.shape[0]
    margin = short_filter.shape[1] - 1
    width = w_proj.shape[2]
    half = width // 2
    chips = lax.axis_size("chip")
    parity = lax.axis_index("core")
    split = w_proj.reshape(w_proj.shape[0], 3, width // (2 * GROUP), 2, GROUP)
    split = jnp.transpose(split, (3, 0, 1, 2, 4)).reshape(1, 2, w_proj.shape[0], 3 * half)
    spread = jnp.broadcast_to(split, (chips,) + split.shape[1:]).reshape((2 * chips,) + split.shape[2:])
    arrived = lax.all_to_all(spread, ("chip", "core"), split_axis=0, concat_axis=0, tiled=True)
    weights = arrived.reshape(2 * chips * w_proj.shape[0], 3 * half)
    stacked = lax.all_gather(tokens, ("core", "mp"), axis=0, tiled=False)
    rows = 2 * rows_dev
    source = jnp.transpose(stacked.reshape(2, -1, rows_dev, tokens.shape[1]), (0, 2, 1, 3)).reshape(rows, -1)
    tail = shifted(source[rows - margin :], "chip", 1)
    extended_tokens = jnp.concatenate([tail, source], axis=0)
    taps = pick(short_filter, 2, parity)
    mixed = []
    projected_all = jnp.dot(extended_tokens, weights, preferred_element_type=jnp.float32)
    for member in range(3):
        projected = projected_all[:, member * half : (member + 1) * half]
        extended = projected.astype(jnp.bfloat16).astype(jnp.float32)
        total = jnp.zeros((rows, half), jnp.float32)
        for offset in range(margin + 1):
            total = total + taps[member, offset][None] * extended[margin - offset : margin - offset + rows]
        mixed.append(total)
    query_rows = mixed[0]
    product = (mixed[1] * mixed[2]).astype(jnp.bfloat16)
    outgoing = product.T.reshape(chips, GROUP, rows)
    arrived = lax.all_to_all(outgoing, "chip", split_axis=0, concat_axis=0, tiled=True)
    convolved = long_conv(arrived, long_filter).astype(jnp.bfloat16)
    returned = lax.all_to_all(convolved, "chip", split_axis=0, concat_axis=0, tiled=True)
    back_rows = returned.reshape(half, rows).T
    gain = pick(skip_gain, 0, parity)
    local = query_rows * (back_rows.astype(jnp.float32) + gain[None, :] * product.astype(jnp.float32))
    local = local.astype(jnp.bfloat16).reshape(2, rows_dev, half)
    swapped = lax.all_to_all(local, "core", split_axis=0, concat_axis=0, tiled=True)
    swapped = swapped.reshape(2, rows_dev, half // GROUP, GROUP)
    return jnp.transpose(swapped, (1, 2, 0, 3)).reshape(rows_dev, width)


def solution(mesh):
    seq_size = mesh.shape["seq"]
    devices = mesh.devices.reshape(seq_size // 2, 2, mesh.shape["mp"])
    inner = jax.sharding.Mesh(devices, ("chip", "core", "mp"))
    seq = ("chip", "core")
    return jax.shard_map(
        on_device,
        mesh=inner,
        in_specs=(
            P(seq, "mp"),
            P(seq, None, "mp"),
            P(None, None, "mp"),
            P(("mp",) + seq, None),
            P("mp"),
        ),
        out_specs=P(seq, "mp"),
        check_vma=False,
    )
```

```python
import numpy as np

import jax
import jax.numpy as jnp
from jax import lax
from jax.sharding import PartitionSpec as P


HIGHEST = lax.Precision.HIGHEST
GROUP = 8


def shifted(value, axis, steps):
    count = lax.axis_size(axis)
    leading, last = (max(0, -steps), min(count, count - steps))
    return lax.ppermute(value, axis, [(source, source + steps) for source in range(leading, last)])


def tables(rows, cols):
    first = np.arange(rows)
    second = np.arange(cols)
    outer = 2.0 * np.pi * np.outer(first, first) / rows
    inner = 2.0 * np.pi * np.outer(second, second) / cols
    twist = 2.0 * np.pi * np.outer(first, second) / (rows * cols)
    f32 = lambda a: jnp.asarray(a.astype(np.float32))
    return dict(
        outer_cos=f32(np.cos(outer)),
        outer_sin=f32(np.sin(outer)),
        inner_cos=f32(np.cos(inner)),
        inner_sin=f32(np.sin(inner)),
        twist_cos=f32(np.cos(twist)),
        twist_sin=f32(np.sin(twist)),
    )


def block(cos, sin, sign):
    return jnp.concatenate(
        [jnp.concatenate([cos, sign * sin], axis=1), jnp.concatenate([-sign * sin, cos], axis=1)], axis=0
    )


def forward(first, t, cols):
    tc = t["twist_cos"][:, None, :]
    ts = t["twist_sin"][:, None, :]
    first_re, first_im = first[..., :cols], first[..., cols:]
    turned = jnp.concatenate([first_re * tc + first_im * ts, first_im * tc - first_re * ts], axis=-1)
    matrix = block(t["inner_cos"], t["inner_sin"], -1.0)
    return jnp.einsum("krn,nm->krm", turned, matrix, precision=HIGHEST)


def long_conv(signal, kernel):
    live, channels, cols = signal.shape
    rows = 2 * live
    t = lax.optimization_barrier(tables(rows, cols))
    first = jnp.concatenate([t["outer_cos"][:, :live], -t["outer_sin"][:, :live]], axis=0)
    own_kernel, own_first, own_t = lax.optimization_barrier((kernel, first, t))
    ker = jnp.einsum("kn,rnm->krm", own_first, own_kernel.reshape(channels, live, cols), precision=HIGHEST)
    ker = jnp.concatenate([ker[:rows], ker[rows:]], axis=-1)
    sh = forward(ker, own_t, cols)
    sig = jnp.einsum("kn,nrm->krm", first, signal.astype(jnp.float32), precision=HIGHEST)
    sig = jnp.concatenate([sig[:rows], sig[rows:]], axis=-1)
    su = forward(sig, t, cols)
    su_re, su_im = su[..., :cols], su[..., cols:]
    sh_re, sh_im = sh[..., :cols], sh[..., cols:]
    z = jnp.concatenate([su_re * sh_re - su_im * sh_im, su_re * sh_im + su_im * sh_re], axis=-1)
    d = jnp.einsum("krn,nm->krm", z, block(t["inner_cos"], t["inner_sin"], 1.0), precision=HIGHEST)
    d_re, d_im = d[..., :cols], d[..., cols:]
    tc = t["twist_cos"][:, None, :]
    ts = t["twist_sin"][:, None, :]
    e = jnp.concatenate([d_re * tc - d_im * ts, d_im * tc + d_re * ts], axis=0)
    scale = 1.0 / (rows * cols)
    back = jnp.concatenate([t["outer_cos"][:live], -t["outer_sin"][:live]], axis=1) * scale
    return jnp.einsum("nk,krm->nrm", back, e, precision=HIGHEST)


def pick(values, axis, parity):
    shape = values.shape
    grouped = values.reshape(shape[:axis] + (shape[axis] // (2 * GROUP), 2, GROUP) + shape[axis + 1 :])
    taken = lax.dynamic_index_in_dim(grouped, parity, axis + 1, keepdims=False)
    return taken.reshape(shape[:axis] + (shape[axis] // 2,) + shape[axis + 1 :])


def layer(tokens, w_proj, short_filter, long_filter, skip_gain):
    rows_dev = tokens.shape[0]
    margin = short_filter.shape[1] - 1
    width = w_proj.shape[2]
    half = width // 2
    chips = lax.axis_size("chip")
    parity = lax.axis_index("core")
    split = w_proj.reshape(w_proj.shape[0], 3, width // (2 * GROUP), 2, GROUP)
    split = jnp.transpose(split, (3, 0, 1, 2, 4)).reshape(1, 2, w_proj.shape[0], 3 * half)
    spread = jnp.broadcast_to(split, (chips,) + split.shape[1:]).reshape((2 * chips,) + split.shape[2:])
    arrived = lax.all_to_all(spread, ("chip", "core"), split_axis=0, concat_axis=0, tiled=True)
    weights = arrived.reshape(2 * chips * w_proj.shape[0], 3 * half)
    stacked = lax.all_gather(tokens, ("core", "mp"), axis=0, tiled=False)
    rows = 2 * rows_dev
    source = jnp.transpose(stacked.reshape(2, -1, rows_dev, tokens.shape[1]), (0, 2, 1, 3)).reshape(rows, -1)
    tail = shifted(source[rows - margin :], "chip", 1)
    extended_tokens = jnp.concatenate([tail, source], axis=0)
    taps = pick(short_filter, 2, parity)
    mixed = []
    projected_all = jnp.dot(extended_tokens, weights, preferred_element_type=jnp.float32)
    for member in range(3):
        projected = projected_all[:, member * half : (member + 1) * half]
        extended = projected.astype(jnp.bfloat16).astype(jnp.float32)
        total = jnp.zeros((rows, half), jnp.float32)
        for offset in range(margin + 1):
            total = total + taps[member, offset][None] * extended[margin - offset : margin - offset + rows]
        mixed.append(total)
    query_rows = mixed[0]
    product = (mixed[1] * mixed[2]).astype(jnp.bfloat16)
    outgoing = product.T.reshape(chips, GROUP, rows)
    arrived = lax.all_to_all(outgoing, "chip", split_axis=0, concat_axis=0, tiled=True)
    convolved = long_conv(arrived, long_filter).astype(jnp.bfloat16)
    returned = lax.all_to_all(convolved, "chip", split_axis=0, concat_axis=0, tiled=True)
    back_rows = returned.reshape(half, rows).T
    gain = pick(skip_gain, 0, parity)
    local = query_rows * (back_rows.astype(jnp.float32) + gain[None, :] * product.astype(jnp.float32))
    local = local.astype(jnp.bfloat16).reshape(2, rows_dev, half)
    swapped = lax.all_to_all(local, "core", split_axis=0, concat_axis=0, tiled=True)
    swapped = swapped.reshape(2, rows_dev, half // GROUP, GROUP)
    return jnp.transpose(swapped, (1, 2, 0, 3)).reshape(rows_dev, width)


def solution(mesh):
    seq_size = mesh.shape["seq"]
    devices = mesh.devices.reshape(seq_size // 2, 2, mesh.shape["mp"])
    inner = jax.sharding.Mesh(devices, ("chip", "core", "mp"))
    seq = ("chip", "core")
    return jax.shard_map(
        layer,
        mesh=inner,
        in_specs=(
            P(seq, "mp"),
            P(seq, None, "mp"),
            P(None, None, "mp"),
            P(("mp",) + seq, None),
            P("mp"),
        ),
        out_specs=P(seq, "mp"),
        check_vma=False,
    )
```

```python
import numpy as np

import jax
import jax.numpy as jnp
from jax import lax
from jax.sharding import PartitionSpec as P


PRECISION = lax.Precision.HIGH
GROUP = 8


def shifted(value, axis, steps):
    count = lax.axis_size(axis)
    leading, last = (max(0, -steps), min(count, count - steps))
    return lax.ppermute(value, axis, [(source, source + steps) for source in range(leading, last)])


def tables(rows, cols):
    first = np.arange(rows)
    second = np.arange(cols)
    outer = 2.0 * np.pi * np.outer(first, first) / rows
    inner = 2.0 * np.pi * np.outer(second, second) / cols
    twist = 2.0 * np.pi * np.outer(first, second) / (rows * cols)
    f32 = lambda a: jnp.asarray(a.astype(np.float32))
    return dict(
        outer_cos=f32(np.cos(outer)),
        outer_sin=f32(np.sin(outer)),
        inner_cos=f32(np.cos(inner)),
        inner_sin=f32(np.sin(inner)),
        twist_cos=f32(np.cos(twist)),
        twist_sin=f32(np.sin(twist)),
    )


def block(cos, sin, sign):
    return jnp.concatenate(
        [jnp.concatenate([cos, sign * sin], axis=1), jnp.concatenate([-sign * sin, cos], axis=1)], axis=0
    )


def forward(first, t, cols):
    tc = t["twist_cos"][:, None, :]
    ts = t["twist_sin"][:, None, :]
    first_re, first_im = first[..., :cols], first[..., cols:]
    turned = jnp.concatenate([first_re * tc + first_im * ts, first_im * tc - first_re * ts], axis=-1)
    matrix = block(t["inner_cos"], t["inner_sin"], -1.0)
    return jnp.einsum("krn,nm->krm", turned, matrix, precision=PRECISION)


def long_conv(signal, kernel):
    live, channels, cols = signal.shape
    rows = 2 * live
    t = lax.optimization_barrier(tables(rows, cols))
    first = jnp.concatenate([t["outer_cos"][:, :live], -t["outer_sin"][:, :live]], axis=0)
    own_kernel, own_first, own_t = lax.optimization_barrier((kernel, first, t))
    ker = jnp.einsum("kn,rnm->krm", own_first, own_kernel.reshape(channels, live, cols), precision=PRECISION)
    ker = jnp.concatenate([ker[:rows], ker[rows:]], axis=-1)
    sh = forward(ker, own_t, cols)
    sig = jnp.einsum("kn,nrm->krm", first, signal.astype(jnp.float32), precision=PRECISION)
    sig = jnp.concatenate([sig[:rows], sig[rows:]], axis=-1)
    su = forward(sig, t, cols)
    su_re, su_im = su[..., :cols], su[..., cols:]
    sh_re, sh_im = sh[..., :cols], sh[..., cols:]
    z = jnp.concatenate([su_re * sh_re - su_im * sh_im, su_re * sh_im + su_im * sh_re], axis=-1)
    d = jnp.einsum("krn,nm->krm", z, block(t["inner_cos"], t["inner_sin"], 1.0), precision=PRECISION)
    d_re, d_im = d[..., :cols], d[..., cols:]
    tc = t["twist_cos"][:, None, :]
    ts = t["twist_sin"][:, None, :]
    e = jnp.concatenate([d_re * tc - d_im * ts, d_im * tc + d_re * ts], axis=0)
    scale = 1.0 / (rows * cols)
    back = jnp.concatenate([t["outer_cos"][:live], -t["outer_sin"][:live]], axis=1) * scale
    return jnp.einsum("nk,krm->nrm", back, e, precision=PRECISION)


def pick(values, axis, parity):
    shape = values.shape
    grouped = values.reshape(shape[:axis] + (shape[axis] // (2 * GROUP), 2, GROUP) + shape[axis + 1 :])
    taken = lax.dynamic_index_in_dim(grouped, parity, axis + 1, keepdims=False)
    return taken.reshape(shape[:axis] + (shape[axis] // 2,) + shape[axis + 1 :])


def layer(tokens, w_proj, short_filter, long_filter, skip_gain):
    rows_dev = tokens.shape[0]
    margin = short_filter.shape[1] - 1
    width = w_proj.shape[2]
    half = width // 2
    chips = lax.axis_size("chip")
    parity = lax.axis_index("core")
    split = w_proj.reshape(w_proj.shape[0], 3, width // (2 * GROUP), 2, GROUP)
    split = jnp.transpose(split, (3, 0, 1, 2, 4)).reshape(1, 2, w_proj.shape[0], 3 * half)
    spread = jnp.broadcast_to(split, (chips,) + split.shape[1:]).reshape((2 * chips,) + split.shape[2:])
    arrived = lax.all_to_all(spread, ("chip", "core"), split_axis=0, concat_axis=0, tiled=True)
    weights = arrived.reshape(2 * chips * w_proj.shape[0], 3 * half)
    stacked = lax.all_gather(tokens, ("core", "mp"), axis=0, tiled=False)
    rows = 2 * rows_dev
    source = jnp.transpose(stacked.reshape(2, -1, rows_dev, tokens.shape[1]), (0, 2, 1, 3)).reshape(rows, -1)
    tail = shifted(source[rows - margin :], "chip", 1)
    extended_tokens = jnp.concatenate([tail, source], axis=0)
    taps = pick(short_filter, 2, parity)
    mixed = []
    projected_all = jnp.dot(extended_tokens, weights, preferred_element_type=jnp.float32)
    for member in range(3):
        projected = projected_all[:, member * half : (member + 1) * half]
        extended = projected.astype(jnp.bfloat16).astype(jnp.float32)
        total = jnp.zeros((rows, half), jnp.float32)
        for offset in range(margin + 1):
            total = total + taps[member, offset][None] * extended[margin - offset : margin - offset + rows]
        mixed.append(total)
    query_rows = mixed[0]
    product = (mixed[1] * mixed[2]).astype(jnp.bfloat16)
    outgoing = product.T.reshape(chips, GROUP, rows)
    arrived = lax.all_to_all(outgoing, "chip", split_axis=0, concat_axis=0, tiled=True)
    convolved = long_conv(arrived, long_filter).astype(jnp.bfloat16)
    returned = lax.all_to_all(convolved, "chip", split_axis=0, concat_axis=0, tiled=True)
    back_rows = returned.reshape(half, rows).T
    gain = pick(skip_gain, 0, parity)
    local = query_rows * (back_rows.astype(jnp.float32) + gain[None, :] * product.astype(jnp.float32))
    local = local.astype(jnp.bfloat16).reshape(2, rows_dev, half)
    swapped = lax.all_to_all(local, "core", split_axis=0, concat_axis=0, tiled=True)
    swapped = swapped.reshape(2, rows_dev, half // GROUP, GROUP)
    return jnp.transpose(swapped, (1, 2, 0, 3)).reshape(rows_dev, width)


def solution(mesh):
    seq_size = mesh.shape["seq"]
    devices = mesh.devices.reshape(seq_size // 2, 2, mesh.shape["mp"])
    inner = jax.sharding.Mesh(devices, ("chip", "core", "mp"))
    seq = ("chip", "core")
    return jax.shard_map(
        layer,
        mesh=inner,
        in_specs=(
            P(seq, "mp"),
            P(seq, None, "mp"),
            P(None, None, "mp"),
            P(("mp",) + seq, None),
            P("mp"),
        ),
        out_specs=P(seq, "mp"),
        check_vma=False,
    )
```

```python
import numpy as np

import jax
import jax.numpy as jnp
from jax import lax
from jax.sharding import PartitionSpec as P


PRECISION = lax.Precision.HIGH
GROUP = 8


def shifted(value, axis, steps):
    count = lax.axis_size(axis)
    leading, last = (max(0, -steps), min(count, count - steps))
    return lax.ppermute(value, axis, [(source, source + steps) for source in range(leading, last)])


def tables(rows, cols):
    first = np.arange(rows)
    second = np.arange(cols)
    outer = 2.0 * np.pi * np.outer(first, first) / rows
    inner = 2.0 * np.pi * np.outer(second, second) / cols
    twist = 2.0 * np.pi * np.outer(first, second) / (rows * cols)
    f32 = lambda a: jnp.asarray(a.astype(np.float32))
    return dict(
        outer_cos=f32(np.cos(outer)),
        outer_sin=f32(np.sin(outer)),
        inner_cos=f32(np.cos(inner)),
        inner_sin=f32(np.sin(inner)),
        twist_cos=f32(np.cos(twist)),
        twist_sin=f32(np.sin(twist)),
    )


def block(cos, sin, sign):
    return jnp.concatenate(
        [jnp.concatenate([cos, sign * sin], axis=1), jnp.concatenate([-sign * sin, cos], axis=1)], axis=0
    )


def forward(first, t, cols):
    tc = t["twist_cos"][:, None, :]
    ts = t["twist_sin"][:, None, :]
    first_re, first_im = first[..., :cols], first[..., cols:]
    turned = jnp.concatenate([first_re * tc + first_im * ts, first_im * tc - first_re * ts], axis=-1)
    matrix = block(t["inner_cos"], t["inner_sin"], -1.0)
    return jnp.einsum("krn,nm->krm", turned, matrix, precision=PRECISION)


def long_conv(signal, kernel):
    live, channels, cols = signal.shape
    rows = 2 * live
    t = lax.optimization_barrier(tables(rows, cols))
    first = jnp.concatenate([t["outer_cos"][:, :live], -t["outer_sin"][:, :live]], axis=0)
    own_kernel, own_first, own_t = lax.optimization_barrier((kernel, first, t))
    ker = jnp.einsum("kn,rnm->krm", own_first, own_kernel.reshape(channels, live, cols), precision=PRECISION)
    ker = jnp.concatenate([ker[:rows], ker[rows:]], axis=-1)
    sh = forward(ker, own_t, cols)
    sig = jnp.einsum("kn,nrm->krm", first, signal.astype(jnp.float32), precision=PRECISION)
    sig = jnp.concatenate([sig[:rows], sig[rows:]], axis=-1)
    su = forward(sig, t, cols)
    su_re, su_im = su[..., :cols], su[..., cols:]
    sh_re, sh_im = sh[..., :cols], sh[..., cols:]
    z = jnp.concatenate([su_re * sh_re - su_im * sh_im, su_re * sh_im + su_im * sh_re], axis=-1)
    d = jnp.einsum("krn,nm->krm", z, block(t["inner_cos"], t["inner_sin"], 1.0), precision=PRECISION)
    d_re, d_im = d[..., :cols], d[..., cols:]
    tc = t["twist_cos"][:, None, :]
    ts = t["twist_sin"][:, None, :]
    e = jnp.concatenate([d_re * tc - d_im * ts, d_im * tc + d_re * ts], axis=0)
    scale = 1.0 / (rows * cols)
    back = jnp.concatenate([t["outer_cos"][:live], -t["outer_sin"][:live]], axis=1) * scale
    return jnp.einsum("nk,krm->nrm", back, e, precision=PRECISION)


def pick(values, axis, parity):
    shape = values.shape
    grouped = values.reshape(shape[:axis] + (shape[axis] // (2 * GROUP), 2, GROUP) + shape[axis + 1 :])
    taken = lax.dynamic_index_in_dim(grouped, parity, axis + 1, keepdims=False)
    return taken.reshape(shape[:axis] + (shape[axis] // 2,) + shape[axis + 1 :])


def layer(tokens, w_proj, short_filter, long_filter, skip_gain):
    rows_dev = tokens.shape[0]
    margin = short_filter.shape[1] - 1
    width = w_proj.shape[2]
    half = width // 2
    chips = lax.axis_size("chip")
    parity = lax.axis_index("core")
    split = w_proj.reshape(w_proj.shape[0], 3, width // (2 * GROUP), 2, GROUP)
    split = jnp.transpose(split, (3, 0, 1, 2, 4)).reshape(2, w_proj.shape[0], 3 * half)
    paired = lax.all_to_all(split, "core", split_axis=0, concat_axis=0, tiled=True)
    paired = paired.reshape(1, 2 * w_proj.shape[0], 3 * half)
    spread = jnp.broadcast_to(paired, (chips,) + paired.shape[1:])
    arrived = lax.all_to_all(spread, "chip", split_axis=0, concat_axis=0, tiled=True)
    weights = arrived.reshape(2 * chips * w_proj.shape[0], 3 * half)
    stacked = lax.all_gather(tokens, ("core", "mp"), axis=0, tiled=False)
    rows = 2 * rows_dev
    source = jnp.transpose(stacked.reshape(2, -1, rows_dev, tokens.shape[1]), (0, 2, 1, 3)).reshape(rows, -1)
    tail = shifted(source[rows - margin :], "chip", 1)
    extended_tokens = jnp.concatenate([tail, source], axis=0)
    taps = pick(short_filter, 2, parity)
    mixed = []
    projected_all = jnp.dot(extended_tokens, weights, preferred_element_type=jnp.float32)
    for member in range(3):
        projected = projected_all[:, member * half : (member + 1) * half]
        extended = projected.astype(jnp.bfloat16).astype(jnp.float32)
        total = jnp.zeros((rows, half), jnp.float32)
        for offset in range(margin + 1):
            total = total + taps[member, offset][None] * extended[margin - offset : margin - offset + rows]
        mixed.append(total)
    query_rows = mixed[0]
    product = (mixed[1] * mixed[2]).astype(jnp.bfloat16)
    outgoing = product.T.reshape(chips, GROUP, rows)
    arrived = lax.all_to_all(outgoing, "chip", split_axis=0, concat_axis=0, tiled=True)
    convolved = long_conv(arrived, long_filter).astype(jnp.bfloat16)
    returned = lax.all_to_all(convolved, "chip", split_axis=0, concat_axis=0, tiled=True)
    back_rows = returned.reshape(half, rows).T
    gain = pick(skip_gain, 0, parity)
    local = query_rows * (back_rows.astype(jnp.float32) + gain[None, :] * product.astype(jnp.float32))
    local = local.astype(jnp.bfloat16).reshape(2, rows_dev, half)
    swapped = lax.all_to_all(local, "core", split_axis=0, concat_axis=0, tiled=True)
    swapped = swapped.reshape(2, rows_dev, half // GROUP, GROUP)
    return jnp.transpose(swapped, (1, 2, 0, 3)).reshape(rows_dev, width)


def solution(mesh):
    seq_size = mesh.shape["seq"]
    devices = mesh.devices.reshape(seq_size // 2, 2, mesh.shape["mp"])
    inner = jax.sharding.Mesh(devices, ("chip", "core", "mp"))
    seq = ("chip", "core")
    return jax.shard_map(
        layer,
        mesh=inner,
        in_specs=(
            P(seq, "mp"),
            P(seq, None, "mp"),
            P(None, None, "mp"),
            P(("mp",) + seq, None),
            P("mp"),
        ),
        out_specs=P(seq, "mp"),
        check_vma=False,
    )
```

```python
import numpy as np

import jax
import jax.numpy as jnp
from jax import lax
from jax.sharding import PartitionSpec as P


PRECISION = lax.Precision.HIGH
GROUP = 8


def shifted(value, axis, steps):
    count = lax.axis_size(axis)
    leading, last = (max(0, -steps), min(count, count - steps))
    return lax.ppermute(value, axis, [(source, source + steps) for source in range(leading, last)])


def tables(rows, cols):
    first = np.arange(rows)
    second = np.arange(cols)
    outer = 2.0 * np.pi * np.outer(first, first) / rows
    inner = 2.0 * np.pi * np.outer(second, second) / cols
    twist = 2.0 * np.pi * np.outer(first, second) / (rows * cols)
    f32 = lambda a: jnp.asarray(a.astype(np.float32))
    return dict(
        outer_cos=f32(np.cos(outer)),
        outer_sin=f32(np.sin(outer)),
        inner_cos=f32(np.cos(inner)),
        inner_sin=f32(np.sin(inner)),
        twist_cos=f32(np.cos(twist)),
        twist_sin=f32(np.sin(twist)),
    )


def block(cos, sin, sign):
    return jnp.concatenate(
        [jnp.concatenate([cos, sign * sin], axis=1), jnp.concatenate([-sign * sin, cos], axis=1)], axis=0
    )


def forward(first, t, cols):
    tc = t["twist_cos"][:, None, :]
    ts = t["twist_sin"][:, None, :]
    first_re, first_im = first[..., :cols], first[..., cols:]
    turned = jnp.concatenate([first_re * tc + first_im * ts, first_im * tc - first_re * ts], axis=-1)
    matrix = block(t["inner_cos"], t["inner_sin"], -1.0)
    return jnp.einsum("krn,nm->krm", turned, matrix, precision=PRECISION)


def long_conv(signal, kernel):
    live, channels, cols = signal.shape
    rows = 2 * live
    t = lax.optimization_barrier(tables(rows, cols))
    first = jnp.concatenate([t["outer_cos"][:, :live], -t["outer_sin"][:, :live]], axis=0)
    own_kernel, own_first, own_t = lax.optimization_barrier((kernel, first, t))
    ker = jnp.einsum("kn,rnm->krm", own_first, own_kernel.reshape(channels, live, cols), precision=PRECISION)
    ker = jnp.concatenate([ker[:rows], ker[rows:]], axis=-1)
    sh = forward(ker, own_t, cols)
    sig = jnp.einsum("kn,nrm->krm", first, signal.astype(jnp.float32), precision=PRECISION)
    sig = jnp.concatenate([sig[:rows], sig[rows:]], axis=-1)
    su = forward(sig, t, cols)
    su_re, su_im = su[..., :cols], su[..., cols:]
    sh_re, sh_im = sh[..., :cols], sh[..., cols:]
    z = jnp.concatenate([su_re * sh_re - su_im * sh_im, su_re * sh_im + su_im * sh_re], axis=-1)
    d = jnp.einsum("krn,nm->krm", z, block(t["inner_cos"], t["inner_sin"], 1.0), precision=PRECISION)
    d_re, d_im = d[..., :cols], d[..., cols:]
    tc = t["twist_cos"][:, None, :]
    ts = t["twist_sin"][:, None, :]
    e = jnp.concatenate([d_re * tc - d_im * ts, d_im * tc + d_re * ts], axis=0)
    scale = 1.0 / (rows * cols)
    back = jnp.concatenate([t["outer_cos"][:live], -t["outer_sin"][:live]], axis=1) * scale
    return jnp.einsum("nk,krm->nrm", back, e, precision=PRECISION)


def pick(values, axis, parity):
    shape = values.shape
    grouped = values.reshape(shape[:axis] + (shape[axis] // (2 * GROUP), 2, GROUP) + shape[axis + 1 :])
    taken = lax.dynamic_index_in_dim(grouped, parity, axis + 1, keepdims=False)
    return taken.reshape(shape[:axis] + (shape[axis] // 2,) + shape[axis + 1 :])


def layer(tokens, w_proj, short_filter, long_filter, skip_gain):
    rows_dev = tokens.shape[0]
    margin = short_filter.shape[1] - 1
    width = w_proj.shape[2]
    half = width // 2
    chips = lax.axis_size("chip")
    parity = lax.axis_index("core")
    split = w_proj.reshape(w_proj.shape[0], 3, width // (2 * GROUP), 2, GROUP)
    split = jnp.transpose(split, (3, 0, 1, 2, 4)).reshape(1, 2, w_proj.shape[0], 3 * half)
    spread = jnp.broadcast_to(split, (chips,) + split.shape[1:]).reshape((2 * chips,) + split.shape[2:])
    arrived = lax.all_to_all(spread, ("chip", "core"), split_axis=0, concat_axis=0, tiled=True)
    weights = arrived.reshape(2 * chips * w_proj.shape[0], 3 * half)
    stacked = lax.all_gather(tokens, ("core", "mp"), axis=0, tiled=False)
    rows = 2 * rows_dev
    source = jnp.transpose(stacked.reshape(2, -1, rows_dev, tokens.shape[1]), (0, 2, 1, 3)).reshape(rows, -1)
    tail = shifted(source[rows - margin :], "chip", 1)
    extended_tokens = jnp.concatenate([tail, source], axis=0)
    taps = pick(short_filter, 2, parity)
    mixed = []
    projected_all = jnp.dot(extended_tokens, weights, preferred_element_type=jnp.float32)
    for member in range(3):
        projected = projected_all[:, member * half : (member + 1) * half]
        extended = projected.astype(jnp.bfloat16).astype(jnp.float32)
        total = jnp.zeros((rows, half), jnp.float32)
        for offset in range(margin + 1):
            total = total + taps[member, offset][None] * extended[margin - offset : margin - offset + rows]
        mixed.append(total)
    query_rows = mixed[0]
    product = (mixed[1] * mixed[2]).astype(jnp.bfloat16)
    outgoing = product.T.reshape(chips, GROUP, rows)
    arrived = lax.all_to_all(outgoing, "chip", split_axis=0, concat_axis=0, tiled=True)
    convolved = long_conv(arrived, long_filter).astype(jnp.bfloat16)
    mine = lambda values: lax.dynamic_slice_in_dim(values, parity * rows_dev, rows_dev, axis=0)
    theirs = lambda values: lax.dynamic_slice_in_dim(values, (1 - parity) * rows_dev, rows_dev, axis=0)
    pairs = [(0, 1), (1, 0)]
    query_other = lax.ppermute(theirs(query_rows), "core", pairs)
    product_other = lax.ppermute(theirs(product), "core", pairs)

    def whole(own, other):
        first = jnp.where(parity == 0, own, other)
        second = jnp.where(parity == 0, other, own)
        both = jnp.stack([first, second]).reshape(2, rows_dev, half // GROUP, GROUP)
        return jnp.transpose(both, (1, 2, 0, 3)).reshape(rows_dev, width)

    query_full = whole(mine(query_rows), query_other)
    product_full = whole(mine(product), product_other).astype(jnp.float32)
    outgoing = convolved.reshape(chips, GROUP, 2, rows_dev).transpose(0, 2, 1, 3).reshape(2 * chips, GROUP, rows_dev)
    returned = lax.all_to_all(outgoing, ("chip", "core"), split_axis=0, concat_axis=0, tiled=True)
    back_rows = returned.reshape(width, rows_dev).T
    result = query_full * (back_rows.astype(jnp.float32) + skip_gain[None, :] * product_full)
    return result.astype(jnp.bfloat16)


def solution(mesh):
    seq_size = mesh.shape["seq"]
    devices = mesh.devices.reshape(seq_size // 2, 2, mesh.shape["mp"])
    inner = jax.sharding.Mesh(devices, ("chip", "core", "mp"))
    seq = ("chip", "core")
    return jax.shard_map(
        layer,
        mesh=inner,
        in_specs=(
            P(seq, "mp"),
            P(seq, None, "mp"),
            P(None, None, "mp"),
            P(("mp",) + seq, None),
            P("mp"),
        ),
        out_specs=P(seq, "mp"),
        check_vma=False,
    )
```

```python
import numpy as np

import jax
import jax.numpy as jnp
from jax import lax
from jax.sharding import PartitionSpec as P


PRECISION = lax.Precision.HIGH
GROUP = 8


def shifted(value, axis, steps):
    count = lax.axis_size(axis)
    leading, last = (max(0, -steps), min(count, count - steps))
    return lax.ppermute(value, axis, [(source, source + steps) for source in range(leading, last)])


def tables(rows, cols):
    first = np.arange(rows)
    second = np.arange(cols)
    outer = 2.0 * np.pi * np.outer(first, first) / rows
    inner = 2.0 * np.pi * np.outer(second, second) / cols
    twist = 2.0 * np.pi * np.outer(first, second) / (rows * cols)
    f32 = lambda a: jnp.asarray(a.astype(np.float32))
    return dict(
        outer_cos=f32(np.cos(outer)),
        outer_sin=f32(np.sin(outer)),
        inner_cos=f32(np.cos(inner)),
        inner_sin=f32(np.sin(inner)),
        twist_cos=f32(np.cos(twist)),
        twist_sin=f32(np.sin(twist)),
    )


def block(cos, sin, sign):
    return jnp.concatenate(
        [jnp.concatenate([cos, sign * sin], axis=1), jnp.concatenate([-sign * sin, cos], axis=1)], axis=0
    )


def forward(first, t, cols):
    tc = t["twist_cos"][:, None, :]
    ts = t["twist_sin"][:, None, :]
    first_re, first_im = first[..., :cols], first[..., cols:]
    turned = jnp.concatenate([first_re * tc + first_im * ts, first_im * tc - first_re * ts], axis=-1)
    matrix = block(t["inner_cos"], t["inner_sin"], -1.0)
    return jnp.einsum("krn,nm->krm", turned, matrix, precision=PRECISION)


def long_conv(signal, kernel):
    live, channels, cols = signal.shape
    rows = 2 * live
    t = lax.optimization_barrier(tables(rows, cols))
    first = jnp.concatenate([t["outer_cos"][:, :live], -t["outer_sin"][:, :live]], axis=0)
    own_kernel, own_first, own_t = lax.optimization_barrier((kernel, first, t))
    ker = jnp.einsum("kn,rnm->krm", own_first, own_kernel.reshape(channels, live, cols), precision=PRECISION)
    ker = jnp.concatenate([ker[:rows], ker[rows:]], axis=-1)
    sh = forward(ker, own_t, cols)
    sig = jnp.einsum("kn,nrm->krm", first, signal.astype(jnp.float32), precision=PRECISION)
    sig = jnp.concatenate([sig[:rows], sig[rows:]], axis=-1)
    su = forward(sig, t, cols)
    su_re, su_im = su[..., :cols], su[..., cols:]
    sh_re, sh_im = sh[..., :cols], sh[..., cols:]
    z = jnp.concatenate([su_re * sh_re - su_im * sh_im, su_re * sh_im + su_im * sh_re], axis=-1)
    d = jnp.einsum("krn,nm->krm", z, block(t["inner_cos"], t["inner_sin"], 1.0), precision=PRECISION)
    d_re, d_im = d[..., :cols], d[..., cols:]
    tc = t["twist_cos"][:, None, :]
    ts = t["twist_sin"][:, None, :]
    e = jnp.concatenate([d_re * tc - d_im * ts, d_im * tc + d_re * ts], axis=0)
    scale = 1.0 / (rows * cols)
    back = jnp.concatenate([t["outer_cos"][:live], -t["outer_sin"][:live]], axis=1) * scale
    return jnp.einsum("nk,krm->nrm", back, e, precision=PRECISION)


def pick(values, axis, parity):
    shape = values.shape
    grouped = values.reshape(shape[:axis] + (shape[axis] // (2 * GROUP), 2, GROUP) + shape[axis + 1 :])
    taken = lax.dynamic_index_in_dim(grouped, parity, axis + 1, keepdims=False)
    return taken.reshape(shape[:axis] + (shape[axis] // 2,) + shape[axis + 1 :])


def layer(tokens, w_proj, short_filter, long_filter, skip_gain):
    rows_dev = tokens.shape[0]
    margin = short_filter.shape[1] - 1
    width = w_proj.shape[2]
    half = width // 2
    chips = lax.axis_size("chip")
    parity = lax.axis_index("core")
    split = w_proj.reshape(w_proj.shape[0], 3, width // (2 * GROUP), 2, GROUP)
    split = jnp.transpose(split, (3, 0, 1, 2, 4)).reshape(1, 2, w_proj.shape[0], 3 * half)
    spread = jnp.broadcast_to(split, (chips,) + split.shape[1:]).reshape((2 * chips,) + split.shape[2:])
    arrived = lax.all_to_all(spread, ("chip", "core"), split_axis=0, concat_axis=0, tiled=True)
    weights = arrived.reshape(2 * chips * w_proj.shape[0], 3 * half)
    stacked = lax.all_gather(tokens, ("core", "mp"), axis=0, tiled=False)
    rows = 2 * rows_dev
    source = jnp.transpose(stacked.reshape(2, -1, rows_dev, tokens.shape[1]), (0, 2, 1, 3)).reshape(rows, -1)
    tail = shifted(source[rows - margin :], "chip", 1)
    extended_tokens = jnp.concatenate([tail, source], axis=0)
    taps = pick(short_filter, 2, parity)

    def branches(columns, members):
        projected_all = jnp.dot(extended_tokens, columns, preferred_element_type=jnp.float32)
        mixed = []
        for index, member in enumerate(members):
            projected = projected_all[:, index * half : (index + 1) * half]
            extended = projected.astype(jnp.bfloat16).astype(jnp.float32)
            total = jnp.zeros((rows, half), jnp.float32)
            for offset in range(margin + 1):
                total = total + taps[member, offset][None] * extended[margin - offset : margin - offset + rows]
            mixed.append(total)
        return mixed

    key_rows, value_rows = branches(weights[:, half:], (1, 2))
    product = (key_rows * value_rows).astype(jnp.bfloat16)
    (query_rows,) = branches(weights[:, :half], (0,))
    outgoing = product.T.reshape(chips, GROUP, rows)
    arrived = lax.all_to_all(outgoing, "chip", split_axis=0, concat_axis=0, tiled=True)
    convolved = long_conv(arrived, long_filter).astype(jnp.bfloat16)
    mine = lambda values: lax.dynamic_slice_in_dim(values, parity * rows_dev, rows_dev, axis=0)
    theirs = lambda values: lax.dynamic_slice_in_dim(values, (1 - parity) * rows_dev, rows_dev, axis=0)
    pairs = [(0, 1), (1, 0)]
    query_other = lax.ppermute(theirs(query_rows), "core", pairs)
    product_other = lax.ppermute(theirs(product), "core", pairs)

    def whole(own, other):
        first = jnp.where(parity == 0, own, other)
        second = jnp.where(parity == 0, other, own)
        both = jnp.stack([first, second]).reshape(2, rows_dev, half // GROUP, GROUP)
        return jnp.transpose(both, (1, 2, 0, 3)).reshape(rows_dev, width)

    query_full = whole(mine(query_rows), query_other)
    product_full = whole(mine(product), product_other).astype(jnp.float32)
    outgoing = convolved.reshape(chips, GROUP, 2, rows_dev).transpose(0, 2, 1, 3).reshape(2 * chips, GROUP, rows_dev)
    returned = lax.all_to_all(outgoing, ("chip", "core"), split_axis=0, concat_axis=0, tiled=True)
    back_rows = returned.reshape(width, rows_dev).T
    result = query_full * (back_rows.astype(jnp.float32) + skip_gain[None, :] * product_full)
    return result.astype(jnp.bfloat16)


def solution(mesh):
    seq_size = mesh.shape["seq"]
    devices = mesh.devices.reshape(seq_size // 2, 2, mesh.shape["mp"])
    inner = jax.sharding.Mesh(devices, ("chip", "core", "mp"))
    seq = ("chip", "core")
    return jax.shard_map(
        layer,
        mesh=inner,
        in_specs=(
            P(seq, "mp"),
            P(seq, None, "mp"),
            P(None, None, "mp"),
            P(("mp",) + seq, None),
            P("mp"),
        ),
        out_specs=P(seq, "mp"),
        check_vma=False,
    )
```
